256 devices in a mesh: seq: 32 (over y, x, core), resp: 8 (over z).
Axes of the slice: x: 4, y: 4, z: 8, core: 2. Of those that a mesh axis runs over, the one named last changes fastest.
Arguments:
- prompt_grad: bfloat16 [32768, 4096], P('seq', 'resp'), may hold values from -0.119628906 to 0.119628906
- prompt_keys: bfloat16 [32768, 128], P('seq'), may hold values from -6 to 6
- prompt_queries: bfloat16 [32768, 128], P('seq'), may hold values from -0.52734375 to 0.52734375
- prompt_decay: float32 [64, 32768], P('resp', 'seq'), may hold values from -2 to 0
- resp_grad: bfloat16 [32768, 4096], P('resp', 'seq'), may hold values from -0.119628906 to 0.119628906
- resp_keys: bfloat16 [32768, 128], P('resp'), may hold values from -6 to 6
- resp_queries: bfloat16 [32768, 128], P('resp'), may hold values from -0.52734375 to 0.52734375
- resp_decay: float32 [64, 32768], P('seq', 'resp'), may hold values from -2 to 0
- resp_segment: int32 [32768], P('resp'), may hold values from 0 to 8, as said below
Outputs:
- prompt_dx: bfloat16 [32768, 4096], P('seq', 'resp')
- resp_dx: bfloat16 [32768, 4096], P('resp', 'seq')
The draws below stay inside these ranges and needn't reach their ends.
Inputs may be any that keep to these rules, and one draw needn't show every extreme that they name: `resp_segment`: each aligned block of 4096 slots holds responses 0 to 7 in this order, each of one slot or more, then padding slots marked 8; a block holds 1024 live slots or more, and some block has no padding.
All inputs are finite; a program needn't handle non-finite values.
Results may differ from the reference program's by a relative error of at most 0.0057.
Values sent between devices are 32-bit elements; how exact they have to be, the bound alone decides.
No kernel may reach another device: no remote copies, remote signals or barrier semaphores. Data moves between devices by JAX's collectives and lax.ppermute only.
A program may use at most 64 MiB of HBM per device.

```python
import math
import jax
import jax.numpy as jnp
from jax import lax

ATTENTION_UNITS = 64
P_SIZE = 64
N = 128
GROUP = 256
PT_DEV = 1024
RT_DEV = 4096
RESP_DEV = 8
PROMPT = 32768
RESP_TOK = 32768


def head_rates(key):
    base_key = jax.random.fold_in(key, 11)
    pick_key, fast_key, slow_key = jax.random.split(base_key, 3)
    fast_count = max(ATTENTION_UNITS // 4, 1)
    order = jax.random.permutation(pick_key, ATTENTION_UNITS)
    is_fast = order < fast_count
    fast_rate = jax.random.uniform(fast_key, (ATTENTION_UNITS,), jnp.float32, 1.0 / 50.0, 1.0 / 30.0)
    slow_rate = jnp.exp(jax.random.uniform(slow_key, (ATTENTION_UNITS,), jnp.float32, math.log(0.3), math.log(8.0))) / PROMPT
    return jnp.where(is_fast, fast_rate, slow_rate)


def decay_field(key, attention_unit_share, length, block_len, salt_value):
    own_key = jax.random.fold_in(key, salt_value)
    jitter_key, scale_key, spot_key, surcharge_seed = jax.random.split(own_key, 4)
    stochastic_perturbation = jax.random.uniform(jitter_key, (ATTENTION_UNITS, length), jnp.float32, 0.4, 1.6)
    block_scale = jnp.exp(jax.random.uniform(scale_key, (ATTENTION_UNITS, length // block_len), jnp.float32, math.log(0.6), math.log(1.5)))
    per_element_granularity = jnp.repeat(block_scale, block_len, axis=1)
    spots = jax.random.randint(spot_key, (2,), 0, length)
    agreement_tally = jnp.sum((jnp.arange(length)[None, :] == spots[:, None]).astype(jnp.float32), axis=0)
    spike_surcharge = jax.random.uniform(surcharge_seed, (ATTENTION_UNITS, 1), jnp.float32, math.log(0.6), math.log(0.8))
    return -attention_unit_share[:, None] * stochastic_perturbation * per_element_granularity + agreement_tally[None, :] * spike_surcharge


def draw_prompt_decay(key, part):
    return decay_field(key, head_rates(key), PROMPT, PT_DEV, 21)


def draw_resp_decay(key, part):
    return decay_field(key, head_rates(key), RESP_TOK, RT_DEV, 31)


def draw_resp_segment(key, part):
    blocks = RESP_TOK // RT_DEV
    live_key, full_key, score_key = jax.random.split(jax.random.fold_in(key, 41), 3)
    live_count = jax.random.randint(live_key, (blocks,), RT_DEV // 4, RT_DEV)
    full_block = jax.random.randint(full_key, (), 0, blocks)
    live_count = live_count.at[full_block].set(RT_DEV)
    live_count = live_count.at[(full_block + 1) % blocks].set(RT_DEV // 2)
    positions = jnp.arange(1, RT_DEV, dtype=jnp.int32)
    scores = jax.random.randint(score_key, (blocks, RT_DEV - 1), 0, 1 << 16) * RT_DEV + positions[None, :]
    scores = jnp.where(positions[None, :] >= live_count[:, None], (1 << 30) + positions[None, :], scores)
    order = jnp.argsort(scores, axis=1)
    cuts = jnp.sort(order[:, :RESP_DEV - 1] + 1, axis=1)
    slots = jnp.arange(RT_DEV, dtype=jnp.int32)
    labels = jnp.sum((cuts[:, None, :] <= slots[None, :, None]).astype(jnp.int32), axis=2)
    labels = jnp.where(slots[None, :] >= live_count[:, None], RESP_DEV, labels)
    return labels.reshape(-1).astype(jnp.int32)


def steps_of(key, shape, shards, smallest, high):
    def one(axis_at, blocks):
        heights = jax.random.uniform(jax.random.fold_in(jax.random.fold_in(key, 6), axis_at), (blocks,), jnp.float32, smallest / len(shards), high / len(shards))
        return jnp.repeat(jnp.exp(heights), shape[axis_at] // blocks).reshape((-1,) + (1,) * (len(shape) - axis_at - 1))

    gain = one(*shards[0])
    for cut in shards[1:]:
        gain = gain * one(*cut)
    return gain


def centred(stream_key, extent, scale, most, shards=(), held_as=jnp.bfloat16):
    level = steps_of(stream_key, extent, shards, -0.22, 0.18) if shards else 1.0
    drawn = jax.random.normal(stream_key, extent, jnp.float32) * scale * level
    return jnp.minimum(jnp.maximum(drawn, -most), most).astype(held_as)


def setup_inputs(seed: int = 0) -> dict:
    streams_of = jax.random.split(jax.random.key(seed), 10)
    return {
        "prompt_grad": centred(streams_of[0], (PROMPT, ATTENTION_UNITS * P_SIZE), 0.02, 0.119628906, ((0, 32), (1, 8))),
        "prompt_keys": centred(streams_of[1], (PROMPT, N), 1.0, 6.0, ((0, 32),)),
        "prompt_queries": centred(streams_of[2], (PROMPT, N), 0.0884, 0.52734375, ((0, 32),)),
        "prompt_decay": draw_prompt_decay(jax.random.fold_in(streams_of[9], 71), 0),
        "resp_grad": centred(streams_of[4], (RESP_TOK, ATTENTION_UNITS * P_SIZE), 0.02, 0.119628906, ((0, 8), (1, 32))),
        "resp_keys": centred(streams_of[5], (RESP_TOK, N), 1.0, 6.0, ((0, 8),)),
        "resp_queries": centred(streams_of[6], (RESP_TOK, N), 0.0884, 0.52734375, ((0, 8),)),
        "resp_decay": draw_resp_decay(jax.random.fold_in(streams_of[9], 71), 0),
        "resp_segment": draw_resp_segment(jax.random.fold_in(streams_of[9], 71), 0),
    }


def rounded(value):
    return lax.optimization_barrier(value.astype(jnp.bfloat16)).astype(jnp.float32)


def group_parts(out_grad, queries, decay, segment, alive_mask):
    tokens = out_grad.shape[0]
    head_count = decay.shape[0]
    groups = tokens // GROUP
    cum_sums = jnp.cumsum(decay, axis=1)
    cum_group = cum_sums.reshape(head_count, groups, GROUP).transpose(1, 0, 2)
    decay_group = decay.reshape(head_count, groups, GROUP).transpose(1, 0, 2)
    before = cum_group[:, :, 0] - decay_group[:, :, 0]
    seg_group = segment.reshape(groups, GROUP)
    alive_group = alive_mask.reshape(groups, GROUP)
    first_label = seg_group[:, 0]
    last_label = seg_group[:, -1]
    grad_group = out_grad.reshape(groups, GROUP, head_count, P_SIZE).astype(jnp.float32)
    query_group = queries.reshape(groups, GROUP, N).astype(jnp.float32)
    keep_mask = (seg_group == first_label[:, None]) & alive_group
    factor = jnp.where(keep_mask[:, None, :], jnp.exp(cum_group - before[:, :, None]), 0.0)
    weighted = rounded(factor.transpose(0, 2, 1)[:, :, :, None] * grad_group)
    states = jnp.einsum('clhp,cln->chpn', weighted, query_group)
    group_gains = jnp.exp(cum_group[:, :, -1] - before)
    joined = (first_label == last_label).astype(jnp.float32)
    linked = jnp.concatenate([jnp.ones((1,), jnp.float32), (last_label[:-1] == first_label[1:]).astype(jnp.float32)])

    def backstep(later_grad, pieces):
        group_state, group_gain, whole_seg, link_flag = pieces
        updated = group_state + (whole_seg * group_gain)[:, None, None] * later_grad
        return link_flag * updated, later_grad

    start_grad, end_grads = lax.scan(backstep, jnp.zeros((head_count, P_SIZE, N), jnp.float32), (states, group_gains, joined, linked), reverse=True)
    return (cum_sums, cum_group, seg_group, alive_group, last_label, grad_group, end_grads, start_grad)


def group_output(key_rows, queries, parts):
    cum_sums, cum_group, seg_group, alive_group, last_label, grad_group, end_grads, start_grad = parts
    groups = seg_group.shape[0]
    head_count = cum_group.shape[1]
    key_group = key_rows.reshape(groups, GROUP, N).astype(jnp.float32)
    query_group = queries.reshape(groups, GROUP, N).astype(jnp.float32)
    scores = jnp.einsum('csn,ctn->cst', query_group, key_group)
    row_index = lax.broadcasted_iota(jnp.int32, (GROUP, GROUP), 0)
    col_index = lax.broadcasted_iota(jnp.int32, (GROUP, GROUP), 1)
    keep_mask = (row_index >= col_index)[None] & (seg_group[:, :, None] == seg_group[:, None, :]) & alive_group[:, :, None]
    spread = cum_group[:, :, :, None] - cum_group[:, :, None, :]
    decays = jnp.exp(jnp.where(keep_mask[:, None], spread, -jnp.inf))
    mixing = rounded(scores[:, None] * decays)
    inner_part = jnp.einsum('chst,cshp->cthp', mixing, grad_group)
    across = jnp.einsum('chpn,ctn->cthp', rounded(end_grads), key_group)
    reach_weight = jnp.where((seg_group == last_label[:, None])[:, None, :], jnp.exp(cum_group[:, :, -1:] - cum_group), 0.0)
    summed_parts = inner_part + across * reach_weight.transpose(0, 2, 1)[:, :, :, None]
    return summed_parts.reshape(groups * GROUP, head_count * P_SIZE)


def initial_state(out_grad, queries, decay, segment, alive_mask, cum_sums):
    tokens = out_grad.shape[0]
    head_count = decay.shape[0]
    firsts = jnp.concatenate([jnp.ones((1,), jnp.bool_), segment[1:] != segment[:-1]])
    labels = jnp.arange(RESP_DEV + 1, dtype=jnp.int32)
    member = segment[:, None] == labels[None, :]
    opening = cum_sums - decay
    base_label = jnp.sum(jnp.where((member & firsts[:, None])[None], opening[:, :, None], 0.0), axis=1)
    base_token = jnp.sum(jnp.where(member[None], base_label[:, None, :], 0.0), axis=2)
    factor = jnp.where(alive_mask[None], jnp.exp(cum_sums - base_token), 0.0)
    weighted = rounded(factor.T[:, :, None] * out_grad.reshape(tokens, head_count, P_SIZE).astype(jnp.float32))
    return jnp.einsum('thp,tn->hpn', weighted, queries.astype(jnp.float32))


def reference(prompt_grad, prompt_keys, prompt_queries, prompt_decay, resp_grad, resp_keys, resp_queries, resp_decay, resp_segment):
    blocks = PROMPT // PT_DEV
    prompt_grads = prompt_grad.reshape(blocks, PT_DEV, ATTENTION_UNITS * P_SIZE)
    prompt_krows = prompt_keys.reshape(blocks, PT_DEV, N)
    prompt_qrows = prompt_queries.reshape(blocks, PT_DEV, N)
    prompt_decays = prompt_decay.reshape(ATTENTION_UNITS, blocks, PT_DEV).transpose(1, 0, 2)
    zero_label = jnp.zeros((PT_DEV,), jnp.int32)
    all_alive = jnp.ones((PT_DEV,), jnp.bool_)

    def prompt_states(pieces):
        grad_block, query_block, decay_block = pieces
        parts = group_parts(grad_block, query_block, decay_block, zero_label, all_alive)
        return parts[7], parts[0][:, -1]

    start_grads, block_totals = lax.map(prompt_states, (prompt_grads, prompt_qrows, prompt_decays))

    resp_blocks = RESP_TOK // RT_DEV
    resp_grads = resp_grad.reshape(resp_blocks, RT_DEV, ATTENTION_UNITS * P_SIZE)
    resp_krows = resp_keys.reshape(resp_blocks, RT_DEV, N)
    resp_qrows = resp_queries.reshape(resp_blocks, RT_DEV, N)
    resp_decays = resp_decay.reshape(ATTENTION_UNITS, resp_blocks, RT_DEV).transpose(1, 0, 2)
    resp_labels = resp_segment.reshape(resp_blocks, RT_DEV)

    def resp_block(pieces):
        grad_block, key_block, query_block, decay_block, label_block = pieces
        alive_block = label_block < RESP_DEV
        parts = group_parts(grad_block, query_block, decay_block, label_block, alive_block)
        local_part = group_output(key_block, query_block, parts)
        init_part = initial_state(grad_block, query_block, decay_block, label_block, alive_block, parts[0])
        return local_part.astype(jnp.bfloat16), init_part

    resp_parts, init_parts = lax.map(resp_block, (resp_grads, resp_krows, resp_qrows, resp_decays, resp_labels))
    resp_init = jnp.sum(init_parts, axis=0)

    def chain_step(later_grad, pieces):
        start_grad, block_total = pieces
        return start_grad + jnp.exp(block_total)[:, None, None] * later_grad, later_grad

    _, incoming = lax.scan(chain_step, resp_init, (start_grads, block_totals), reverse=True)

    def prompt_block(pieces):
        grad_block, key_block, query_block, decay_block, enter_grad = pieces
        parts = group_parts(grad_block, query_block, decay_block, zero_label, all_alive)
        local_part = group_output(key_block, query_block, parts)
        cum_sums = parts[0]
        carry_term = jnp.einsum('hpn,tn->thp', rounded(enter_grad), key_block.astype(jnp.float32))
        carry_term = carry_term * jnp.exp(cum_sums[:, -1:] - cum_sums).T[:, :, None]
        return (local_part + carry_term.reshape(PT_DEV, ATTENTION_UNITS * P_SIZE)).astype(jnp.bfloat16)

    prompt_out = lax.map(prompt_block, (prompt_grads, prompt_krows, prompt_qrows, prompt_decays, incoming))
    return prompt_out.reshape(PROMPT, ATTENTION_UNITS * P_SIZE), resp_parts.reshape(RESP_TOK, ATTENTION_UNITS * P_SIZE)
```

```python
import jax
import jax.numpy as jnp
from jax import lax
from jax.sharding import PartitionSpec as P

P_SIZE = 64
N = 128
GROUP = 256
RESP_DEV = 8


def group_parts(out_grad, queries, decay, segment, alive_mask):
    tokens = out_grad.shape[0]
    head_count = decay.shape[0]
    groups = tokens // GROUP
    cum_sums = jnp.cumsum(decay, axis=1)
    cum_group = cum_sums.reshape(head_count, groups, GROUP).transpose(1, 0, 2)
    decay_group = decay.reshape(head_count, groups, GROUP).transpose(1, 0, 2)
    before = cum_group[:, :, 0] - decay_group[:, :, 0]
    seg_group = segment.reshape(groups, GROUP)
    alive_group = alive_mask.reshape(groups, GROUP)
    first_label = seg_group[:, 0]
    last_label = seg_group[:, -1]
    grad_group = out_grad.reshape(groups, GROUP, head_count, P_SIZE)
    query_group = queries.reshape(groups, GROUP, N)
    keep_mask = (seg_group == first_label[:, None]) & alive_group
    factor = jnp.where(keep_mask[:, None, :], jnp.exp(cum_group - before[:, :, None]), 0.0)
    weighted = (factor.transpose(0, 2, 1)[:, :, :, None] * grad_group).astype(jnp.bfloat16)
    states = jnp.einsum("clhp,cln->chpn", weighted, query_group, preferred_element_type=jnp.float32)
    group_gains = jnp.exp(cum_group[:, :, -1] - before)
    joined = (first_label == last_label).astype(jnp.float32)
    linked = jnp.concatenate(
        [jnp.ones((1,), jnp.float32), (last_label[:-1] == first_label[1:]).astype(jnp.float32)]
    )

    flow = joined[:, None] * group_gains * jnp.concatenate(
        [linked[1:], jnp.zeros((1,), jnp.float32)]
    )[:, None]
    carry_at = jnp.arange(groups + 1)[:, None, None]
    state_at = jnp.arange(groups)[None, :, None]
    step_at = jnp.arange(groups)[None, None, :]
    inside = (carry_at <= step_at) & (step_at < state_at)
    spans = jnp.prod(jnp.where(inside[None], flow.T[:, None, None, :], 1.0), axis=3)
    link_at = jnp.concatenate([linked, jnp.zeros((1,), jnp.float32)])
    coef = jnp.where((carry_at[:, :, 0] <= state_at[:, :, 0])[None], spans, 0.0) * link_at[None, :, None]
    carries = jnp.einsum(
        "hcd,dhpn->chpn", coef, states, precision=lax.Precision.HIGHEST
    )
    start_grad = carries[0]
    end_grads = carries[1:]
    return (
        cum_sums,
        cum_group,
        seg_group,
        alive_group,
        last_label,
        grad_group,
        end_grads,
        start_grad,
    )


def group_output(key_rows, queries, parts):
    cum_sums, cum_group, seg_group, alive_group, last_label, grad_group, end_grads, start_grad = (
        parts
    )
    groups = seg_group.shape[0]
    head_count = cum_group.shape[1]
    key_group = key_rows.reshape(groups, GROUP, N)
    query_group = queries.reshape(groups, GROUP, N)
    scores = jnp.einsum("csn,ctn->cst", query_group, key_group, preferred_element_type=jnp.float32)
    row_index = lax.broadcasted_iota(jnp.int32, (GROUP, GROUP), 0)
    col_index = lax.broadcasted_iota(jnp.int32, (GROUP, GROUP), 1)
    keep_mask = (
        (row_index >= col_index)[None]
        & (seg_group[:, :, None] == seg_group[:, None, :])
        & alive_group[:, :, None]
    )
    spread = cum_group[:, :, :, None] - cum_group[:, :, None, :]
    decays = jnp.exp(jnp.where(keep_mask[:, None], spread, -jnp.inf))
    mixing = (scores[:, None] * decays).astype(jnp.bfloat16)
    inner_part = jnp.einsum(
        "chst,cshp->cthp", mixing, grad_group, preferred_element_type=jnp.float32
    )
    across = jnp.einsum(
        "chpn,ctn->cthp",
        end_grads.astype(jnp.bfloat16),
        key_group,
        preferred_element_type=jnp.float32,
    )
    reach_weight = jnp.where(
        (seg_group == last_label[:, None])[:, None, :],
        jnp.exp(cum_group[:, :, -1:] - cum_group),
        0.0,
    )
    summed_parts = inner_part + across * reach_weight.transpose(0, 2, 1)[:, :, :, None]
    return summed_parts.reshape(groups * GROUP, head_count * P_SIZE)


def initial_state(out_grad, queries, decay, segment, alive_mask, cum_sums):
    tokens = out_grad.shape[0]
    head_count = decay.shape[0]
    firsts = jnp.concatenate([jnp.ones((1,), jnp.bool_), segment[1:] != segment[:-1]])
    labels = jnp.arange(RESP_DEV + 1, dtype=jnp.int32)
    member = segment[:, None] == labels[None, :]
    opening = cum_sums - decay
    base_label = jnp.sum(
        jnp.where((member & firsts[:, None])[None], opening[:, :, None], 0.0), axis=1
    )
    base_token = jnp.sum(jnp.where(member[None], base_label[:, None, :], 0.0), axis=2)
    factor = jnp.where(alive_mask[None], jnp.exp(cum_sums - base_token), 0.0)
    weighted = (factor.T[:, :, None] * out_grad.reshape(tokens, head_count, P_SIZE)).astype(
        jnp.bfloat16
    )
    return jnp.einsum("thp,tn->hpn", weighted, queries, preferred_element_type=jnp.float32)


def on_device(
    prompt_grad,
    prompt_keys,
    prompt_queries,
    prompt_decay,
    resp_grad,
    resp_keys,
    resp_queries,
    resp_decay,
    resp_segment,
):
    resp_alive = resp_segment < RESP_DEV
    resp_parts = group_parts(resp_grad, resp_queries, resp_decay, resp_segment, resp_alive)
    resp_dx = group_output(resp_keys, resp_queries, resp_parts).astype(jnp.bfloat16)
    partial_state = initial_state(
        resp_grad, resp_queries, resp_decay, resp_segment, resp_alive, resp_parts[0]
    )
    summed_state = lax.psum(partial_state, "resp")
    head_count = prompt_decay.shape[0]
    prompt_len = prompt_grad.shape[0]
    zero_label = jnp.zeros((prompt_len,), jnp.int32)
    all_alive = jnp.ones((prompt_len,), jnp.bool_)
    prompt_parts = group_parts(prompt_grad, prompt_queries, prompt_decay, zero_label, all_alive)
    cum_sums = prompt_parts[0]
    start_grad = prompt_parts[7]
    shard_total = cum_sums[:, -1]
    seq_index = lax.axis_index("seq")
    resp_index = lax.axis_index("resp")
    first_head = seq_index * summed_state.shape[0]
    owned = first_head // head_count == resp_index
    slots = lax.dynamic_update_slice_in_dim(
        jnp.zeros((head_count,) + summed_state.shape[1:], jnp.float32),
        summed_state,
        first_head % head_count,
        0,
    )
    my_heads = lax.psum(jnp.where(owned, slots, 0.0), "seq")
    span_len = lax.axis_size("seq")
    whole_b = start_grad
    whole_a = jnp.exp(shard_total)
    later_b = jnp.zeros_like(start_grad)
    later_a = jnp.ones_like(whole_a)
    shift = 1
    while shift < span_len:
        pairs = [(k + shift, k) for k in range(span_len - shift)]
        message = jnp.concatenate(
            [whole_b, jnp.broadcast_to(whole_a[:, None, None], (head_count, 1, N))], axis=1
        )
        got = lax.ppermute(message, "seq", pairs)
        valid = seq_index + shift < span_len
        got_b = jnp.where(valid, got[:, :P_SIZE], 0.0)
        got_a = jnp.where(valid, got[:, P_SIZE, 0], 1.0)
        later_b = later_b + later_a[:, None, None] * got_b
        later_a = later_a * got_a
        if shift * 2 < span_len:
            whole_b = whole_b + whole_a[:, None, None] * got_b
            whole_a = whole_a * got_a
        shift *= 2
    incoming = later_b + later_a[:, None, None] * my_heads
    local_part = group_output(prompt_keys, prompt_queries, prompt_parts)
    carry_term = jnp.einsum(
        "hpn,tn->thp",
        incoming.astype(jnp.bfloat16),
        prompt_keys,
        preferred_element_type=jnp.float32,
    )
    carry_term = carry_term * jnp.exp(shard_total[:, None] - cum_sums).T[:, :, None]
    prompt_dx = (local_part + carry_term.reshape(prompt_len, head_count * P_SIZE)).astype(
        jnp.bfloat16
    )
    return (prompt_dx, resp_dx)


def solution(mesh):
    return jax.shard_map(
        on_device,
        mesh=mesh,
        in_specs=(
            P("seq", "resp"),
            P("seq", None),
            P("seq", None),
            P("resp", "seq"),
            P("resp", "seq"),
            P("resp", None),
            P("resp", None),
            P("seq", "resp"),
            P("resp"),
        ),
        out_specs=(P("seq", "resp"), P("resp", "seq")),
        check_vma=False,
    )
```

```python
import jax
import jax.numpy as jnp
from jax import lax
from jax.sharding import PartitionSpec as P

P_SIZE = 64
N = 128
GROUP = 256
RESP_DEV = 8


def group_parts(out_grad, queries, decay, segment, alive_mask):
    tokens = out_grad.shape[0]
    head_count = decay.shape[0]
    groups = tokens // GROUP
    cum_sums = jnp.cumsum(decay, axis=1)
    cum_group = cum_sums.reshape(head_count, groups, GROUP).transpose(1, 0, 2)
    decay_group = decay.reshape(head_count, groups, GROUP).transpose(1, 0, 2)
    before = cum_group[:, :, 0] - decay_group[:, :, 0]
    seg_group = segment.reshape(groups, GROUP)
    alive_group = alive_mask.reshape(groups, GROUP)
    first_label = seg_group[:, 0]
    last_label = seg_group[:, -1]
    grad_group = out_grad.reshape(groups, GROUP, head_count, P_SIZE)
    query_group = queries.reshape(groups, GROUP, N)
    keep_mask = (seg_group == first_label[:, None]) & alive_group
    factor = jnp.where(keep_mask[:, None, :], jnp.exp(cum_group - before[:, :, None]), 0.0)
    weighted = (factor.transpose(0, 2, 1)[:, :, :, None] * grad_group).astype(jnp.bfloat16)
    states = jnp.einsum("clhp,cln->chpn", weighted, query_group, preferred_element_type=jnp.float32)
    group_gains = jnp.exp(cum_group[:, :, -1] - before)
    joined = (first_label == last_label).astype(jnp.float32)
    linked = jnp.concatenate(
        [jnp.ones((1,), jnp.float32), (last_label[:-1] == first_label[1:]).astype(jnp.float32)]
    )

    flow = joined[:, None] * group_gains * jnp.concatenate(
        [linked[1:], jnp.zeros((1,), jnp.float32)]
    )[:, None]
    carry_at = jnp.arange(groups + 1)[:, None, None]
    state_at = jnp.arange(groups)[None, :, None]
    step_at = jnp.arange(groups)[None, None, :]
    inside = (carry_at <= step_at) & (step_at < state_at)
    spans = jnp.prod(jnp.where(inside[None], flow.T[:, None, None, :], 1.0), axis=3)
    link_at = jnp.concatenate([linked, jnp.zeros((1,), jnp.float32)])
    coef = jnp.where((carry_at[:, :, 0] <= state_at[:, :, 0])[None], spans, 0.0) * link_at[None, :, None]
    carries = jnp.einsum(
        "hcd,dhpn->chpn", coef, states, precision=lax.Precision.HIGHEST
    )
    start_grad = carries[0]
    end_grads = carries[1:]
    return (
        cum_sums,
        cum_group,
        seg_group,
        alive_group,
        last_label,
        grad_group,
        end_grads,
        start_grad,
    )


def group_output(key_rows, queries, parts):
    cum_sums, cum_group, seg_group, alive_group, last_label, grad_group, end_grads, start_grad = (
        parts
    )
    groups = seg_group.shape[0]
    head_count = cum_group.shape[1]
    key_group = key_rows.reshape(groups, GROUP, N)
    query_group = queries.reshape(groups, GROUP, N)
    scores = jnp.einsum("csn,ctn->cst", query_group, key_group, preferred_element_type=jnp.float32)
    row_index = lax.broadcasted_iota(jnp.int32, (GROUP, GROUP), 0)
    col_index = lax.broadcasted_iota(jnp.int32, (GROUP, GROUP), 1)
    keep_mask = (
        (row_index >= col_index)[None]
        & (seg_group[:, :, None] == seg_group[:, None, :])
        & alive_group[:, :, None]
    )
    spread = cum_group[:, :, :, None] - cum_group[:, :, None, :]
    decays = jnp.exp(jnp.where(keep_mask[:, None], spread, -jnp.inf))
    mixing = (scores[:, None] * decays).astype(jnp.bfloat16)
    inner_part = jnp.einsum(
        "chst,cshp->cthp", mixing, grad_group, preferred_element_type=jnp.float32
    )
    across = jnp.einsum(
        "chpn,ctn->cthp",
        end_grads.astype(jnp.bfloat16),
        key_group,
        preferred_element_type=jnp.float32,
    )
    reach_weight = jnp.where(
        (seg_group == last_label[:, None])[:, None, :],
        jnp.exp(cum_group[:, :, -1:] - cum_group),
        0.0,
    )
    summed_parts = inner_part + across * reach_weight.transpose(0, 2, 1)[:, :, :, None]
    return summed_parts.reshape(groups * GROUP, head_count * P_SIZE)


def initial_state(out_grad, queries, decay, segment, alive_mask, cum_sums):
    tokens = out_grad.shape[0]
    head_count = decay.shape[0]
    firsts = jnp.concatenate([jnp.ones((1,), jnp.bool_), segment[1:] != segment[:-1]])
    labels = jnp.arange(RESP_DEV + 1, dtype=jnp.int32)
    member = segment[:, None] == labels[None, :]
    opening = cum_sums - decay
    base_label = jnp.sum(
        jnp.where((member & firsts[:, None])[None], opening[:, :, None], 0.0), axis=1
    )
    base_token = jnp.sum(jnp.where(member[None], base_label[:, None, :], 0.0), axis=2)
    factor = jnp.where(alive_mask[None], jnp.exp(cum_sums - base_token), 0.0)
    weighted = (factor.T[:, :, None] * out_grad.reshape(tokens, head_count, P_SIZE)).astype(
        jnp.bfloat16
    )
    return jnp.einsum("thp,tn->hpn", weighted, queries, preferred_element_type=jnp.float32)


def on_device(
    prompt_grad,
    prompt_keys,
    prompt_queries,
    prompt_decay,
    resp_grad,
    resp_keys,
    resp_queries,
    resp_decay,
    resp_segment,
):
    resp_alive = resp_segment < RESP_DEV
    resp_parts = group_parts(resp_grad, resp_queries, resp_decay, resp_segment, resp_alive)
    resp_dx = group_output(resp_keys, resp_queries, resp_parts).astype(jnp.bfloat16)
    partial_state = initial_state(
        resp_grad, resp_queries, resp_decay, resp_segment, resp_alive, resp_parts[0]
    )
    resp_len = lax.axis_size("resp")
    shift = 1
    summed_state = partial_state
    while shift < resp_len:
        summed_state = summed_state + lax.ppermute(
            summed_state, "resp", [(k, k ^ shift) for k in range(resp_len)]
        )
        shift *= 2
    head_count = prompt_decay.shape[0]
    prompt_len = prompt_grad.shape[0]
    zero_label = jnp.zeros((prompt_len,), jnp.int32)
    all_alive = jnp.ones((prompt_len,), jnp.bool_)
    prompt_parts = group_parts(prompt_grad, prompt_queries, prompt_decay, zero_label, all_alive)
    cum_sums = prompt_parts[0]
    start_grad = prompt_parts[7]
    shard_total = cum_sums[:, -1]
    seq_index = lax.axis_index("seq")
    seq_len = lax.axis_size("seq")
    share = head_count // summed_state.shape[0]
    pieces = []
    for turn in range(share):
        pairs = []
        for src_seq in range(seq_len):
            for src_resp in range(resp_len):
                dst_seq = share * src_resp + (src_seq % share + turn) % share
                dst_resp = src_seq // share
                pairs.append((src_seq * resp_len + src_resp, dst_seq * resp_len + dst_resp))
        pieces.append(lax.ppermute(summed_state, ("seq", "resp"), pairs))
    pieces = jnp.stack(pieces)
    order = (seq_index % share - jnp.arange(share)) % share
    my_heads = jnp.take(pieces, order, axis=0).reshape((head_count,) + summed_state.shape[1:])
    span_len = lax.axis_size("seq")
    whole_b = start_grad
    whole_a = jnp.exp(shard_total)
    later_b = jnp.zeros_like(start_grad)
    later_a = jnp.ones_like(whole_a)
    shift = 1
    while shift < span_len:
        pairs = [(k + shift, k) for k in range(span_len - shift)]
        message = jnp.concatenate(
            [whole_b, jnp.broadcast_to(whole_a[:, None, None], (head_count, 1, N))], axis=1
        )
        got = lax.ppermute(message, "seq", pairs)
        valid = seq_index + shift < span_len
        got_b = jnp.where(valid, got[:, :P_SIZE], 0.0)
        got_a = jnp.where(valid, got[:, P_SIZE, 0], 1.0)
        later_b = later_b + later_a[:, None, None] * got_b
        later_a = later_a * got_a
        if shift * 2 < span_len:
            whole_b = whole_b + whole_a[:, None, None] * got_b
            whole_a = whole_a * got_a
        shift *= 2
    incoming = later_b + later_a[:, None, None] * my_heads
    local_part = group_output(prompt_keys, prompt_queries, prompt_parts)
    carry_term = jnp.einsum(
        "hpn,tn->thp",
        incoming.astype(jnp.bfloat16),
        prompt_keys,
        preferred_element_type=jnp.float32,
    )
    carry_term = carry_term * jnp.exp(shard_total[:, None] - cum_sums).T[:, :, None]
    prompt_dx = (local_part + carry_term.reshape(prompt_len, head_count * P_SIZE)).astype(
        jnp.bfloat16
    )
    return (prompt_dx, resp_dx)


def solution(mesh):
    return jax.shard_map(
        on_device,
        mesh=mesh,
        in_specs=(
            P("seq", "resp"),
            P("seq", None),
            P("seq", None),
            P("resp", "seq"),
            P("resp", "seq"),
            P("resp", None),
            P("resp", None),
            P("seq", "resp"),
            P("resp"),
        ),
        out_specs=(P("seq", "resp"), P("resp", "seq")),
        check_vma=False,
    )
```

```python
import jax
import jax.numpy as jnp
from jax import lax
from jax.sharding import PartitionSpec as P

P_SIZE = 64
N = 128
GROUP = 256
RESP_DEV = 8


def group_parts(out_grad, queries, decay, segment, alive_mask):
    tokens = out_grad.shape[0]
    head_count = decay.shape[0]
    groups = tokens // GROUP
    cum_sums = jnp.cumsum(decay, axis=1)
    cum_group = cum_sums.reshape(head_count, groups, GROUP).transpose(1, 0, 2)
    decay_group = decay.reshape(head_count, groups, GROUP).transpose(1, 0, 2)
    before = cum_group[:, :, 0] - decay_group[:, :, 0]
    seg_group = segment.reshape(groups, GROUP)
    alive_group = alive_mask.reshape(groups, GROUP)
    first_label = seg_group[:, 0]
    last_label = seg_group[:, -1]
    grad_group = out_grad.reshape(groups, GROUP, head_count, P_SIZE)
    query_group = queries.reshape(groups, GROUP, N)
    keep_mask = (seg_group == first_label[:, None]) & alive_group
    factor = jnp.where(keep_mask[:, None, :], jnp.exp(cum_group - before[:, :, None]), 0.0)
    weighted = (factor.transpose(0, 2, 1)[:, :, :, None] * grad_group).astype(jnp.bfloat16)
    states = jnp.einsum("clhp,cln->chpn", weighted, query_group, preferred_element_type=jnp.float32)
    group_gains = jnp.exp(cum_group[:, :, -1] - before)
    joined = (first_label == last_label).astype(jnp.float32)
    linked = jnp.concatenate(
        [jnp.ones((1,), jnp.float32), (last_label[:-1] == first_label[1:]).astype(jnp.float32)]
    )

    flow = joined[:, None] * group_gains * jnp.concatenate(
        [linked[1:], jnp.zeros((1,), jnp.float32)]
    )[:, None]
    carry_at = jnp.arange(groups + 1)[:, None, None]
    state_at = jnp.arange(groups)[None, :, None]
    step_at = jnp.arange(groups)[None, None, :]
    inside = (carry_at <= step_at) & (step_at < state_at)
    spans = jnp.prod(jnp.where(inside[None], flow.T[:, None, None, :], 1.0), axis=3)
    link_at = jnp.concatenate([linked, jnp.zeros((1,), jnp.float32)])
    coef = jnp.where((carry_at[:, :, 0] <= state_at[:, :, 0])[None], spans, 0.0) * link_at[None, :, None]
    carries = jnp.einsum(
        "hcd,dhpn->chpn", coef, states, precision=lax.Precision.HIGHEST
    )
    start_grad = carries[0]
    end_grads = carries[1:]
    return (
        cum_sums,
        cum_group,
        seg_group,
        alive_group,
        last_label,
        grad_group,
        end_grads,
        start_grad,
    )


def group_output(key_rows, queries, parts):
    cum_sums, cum_group, seg_group, alive_group, last_label, grad_group, end_grads, start_grad = (
        parts
    )
    groups = seg_group.shape[0]
    head_count = cum_group.shape[1]
    key_group = key_rows.reshape(groups, GROUP, N)
    query_group = queries.reshape(groups, GROUP, N)
    scores = jnp.einsum("csn,ctn->cst", query_group, key_group, preferred_element_type=jnp.float32)
    row_index = lax.broadcasted_iota(jnp.int32, (GROUP, GROUP), 0)
    col_index = lax.broadcasted_iota(jnp.int32, (GROUP, GROUP), 1)
    keep_mask = (
        (row_index >= col_index)[None]
        & (seg_group[:, :, None] == seg_group[:, None, :])
        & alive_group[:, :, None]
    )
    spread = cum_group[:, :, :, None] - cum_group[:, :, None, :]
    decays = jnp.exp(jnp.where(keep_mask[:, None], spread, -jnp.inf))
    mixing = (scores[:, None] * decays).astype(jnp.bfloat16)
    inner_part = jnp.einsum(
        "chst,cshp->cthp", mixing, grad_group, preferred_element_type=jnp.float32
    )
    across = jnp.einsum(
        "chpn,ctn->cthp",
        end_grads.astype(jnp.bfloat16),
        key_group,
        preferred_element_type=jnp.float32,
    )
    reach_weight = jnp.where(
        (seg_group == last_label[:, None])[:, None, :],
        jnp.exp(cum_group[:, :, -1:] - cum_group),
        0.0,
    )
    summed_parts = inner_part + across * reach_weight.transpose(0, 2, 1)[:, :, :, None]
    return summed_parts.reshape(groups * GROUP, head_count * P_SIZE)


def initial_state(out_grad, queries, decay, segment, alive_mask, cum_sums):
    tokens = out_grad.shape[0]
    head_count = decay.shape[0]
    firsts = jnp.concatenate([jnp.ones((1,), jnp.bool_), segment[1:] != segment[:-1]])
    labels = jnp.arange(RESP_DEV + 1, dtype=jnp.int32)
    member = segment[:, None] == labels[None, :]
    opening = cum_sums - decay
    base_label = jnp.sum(
        jnp.where((member & firsts[:, None])[None], opening[:, :, None], 0.0), axis=1
    )
    base_token = jnp.sum(jnp.where(member[None], base_label[:, None, :], 0.0), axis=2)
    factor = jnp.where(alive_mask[None], jnp.exp(cum_sums - base_token), 0.0)
    weighted = (factor.T[:, :, None] * out_grad.reshape(tokens, head_count, P_SIZE)).astype(
        jnp.bfloat16
    )
    return jnp.einsum("thp,tn->hpn", weighted, queries, preferred_element_type=jnp.float32)


def on_device(
    prompt_grad,
    prompt_keys,
    prompt_queries,
    prompt_decay,
    resp_grad,
    resp_keys,
    resp_queries,
    resp_decay,
    resp_segment,
):
    resp_alive = resp_segment < RESP_DEV
    resp_parts = group_parts(resp_grad, resp_queries, resp_decay, resp_segment, resp_alive)
    resp_dx = group_output(resp_keys, resp_queries, resp_parts).astype(jnp.bfloat16)
    partial_state = initial_state(
        resp_grad, resp_queries, resp_decay, resp_segment, resp_alive, resp_parts[0]
    )
    resp_len = lax.axis_size("resp")
    head_count = prompt_decay.shape[0]
    prompt_len = prompt_grad.shape[0]
    zero_label = jnp.zeros((prompt_len,), jnp.int32)
    all_alive = jnp.ones((prompt_len,), jnp.bool_)
    prompt_parts = group_parts(prompt_grad, prompt_queries, prompt_decay, zero_label, all_alive)
    cum_sums = prompt_parts[0]
    start_grad = prompt_parts[7]
    shard_total = cum_sums[:, -1]
    seq_index = lax.axis_index("seq")
    seq_len = lax.axis_size("seq")
    share = head_count // partial_state.shape[0]
    pieces = []
    for turn in range(share):
        pairs = []
        for src_seq in range(seq_len):
            for src_resp in range(resp_len):
                dst_seq = share * src_resp + (src_seq % share + turn) % share
                dst_resp = src_seq // share
                pairs.append((src_seq * resp_len + src_resp, dst_seq * resp_len + dst_resp))
        pieces.append(lax.ppermute(partial_state, ("seq", "resp"), pairs))
    pieces = jnp.stack(pieces)
    order = (seq_index % share - jnp.arange(share)) % share
    my_heads = jnp.take(pieces, order, axis=0).reshape((head_count,) + partial_state.shape[1:])
    whole_b = start_grad
    whole_a = jnp.exp(shard_total)
    later_b = jnp.zeros_like(start_grad)
    later_a = jnp.ones_like(whole_a)
    shift = 1
    while shift < seq_len:
        pairs = [((k + shift) % seq_len, k) for k in range(seq_len)]
        parts = [whole_b, jnp.broadcast_to(whole_a[:, None, None], (head_count, 1, N))]
        if shift >= share:
            parts.append(my_heads)
        got = lax.ppermute(jnp.concatenate(parts, axis=1), "seq", pairs)
        valid = seq_index + shift < seq_len
        got_b = jnp.where(valid, got[:, :P_SIZE], 0.0)
        got_a = jnp.where(valid, got[:, P_SIZE, 0], 1.0)
        if shift >= share:
            my_heads = my_heads + got[:, P_SIZE + 1 :]
        later_b = later_b + later_a[:, None, None] * got_b
        later_a = later_a * got_a
        if shift * 2 < seq_len:
            whole_b = whole_b + whole_a[:, None, None] * got_b
            whole_a = whole_a * got_a
        shift *= 2
    incoming = later_b + later_a[:, None, None] * my_heads
    local_part = group_output(prompt_keys, prompt_queries, prompt_parts)
    carry_term = jnp.einsum(
        "hpn,tn->thp",
        incoming.astype(jnp.bfloat16),
        prompt_keys,
        preferred_element_type=jnp.float32,
    )
    carry_term = carry_term * jnp.exp(shard_total[:, None] - cum_sums).T[:, :, None]
    prompt_dx = (local_part + carry_term.reshape(prompt_len, head_count * P_SIZE)).astype(
        jnp.bfloat16
    )
    return (prompt_dx, resp_dx)


def solution(mesh):
    return jax.shard_map(
        on_device,
        mesh=mesh,
        in_specs=(
            P("seq", "resp"),
            P("seq", None),
            P("seq", None),
            P("resp", "seq"),
            P("resp", "seq"),
            P("resp", None),
            P("resp", None),
            P("seq", "resp"),
            P("resp"),
        ),
        out_specs=(P("seq", "resp"), P("resp", "seq")),
        check_vma=False,
    )
```

```python
import jax
import jax.numpy as jnp
from jax import lax
from jax.sharding import PartitionSpec as P

P_SIZE = 64
N = 128
GROUP = 256
RESP_DEV = 8


def group_parts(out_grad, queries, decay, segment, alive_mask):
    tokens = out_grad.shape[0]
    head_count = decay.shape[0]
    groups = tokens // GROUP
    cum_sums = jnp.cumsum(decay, axis=1)
    cum_group = cum_sums.reshape(head_count, groups, GROUP).transpose(1, 0, 2)
    decay_group = decay.reshape(head_count, groups, GROUP).transpose(1, 0, 2)
    before = cum_group[:, :, 0] - decay_group[:, :, 0]
    seg_group = segment.reshape(groups, GROUP)
    alive_group = alive_mask.reshape(groups, GROUP)
    first_label = seg_group[:, 0]
    last_label = seg_group[:, -1]
    grad_group = out_grad.reshape(groups, GROUP, head_count, P_SIZE)
    query_group = queries.reshape(groups, GROUP, N)
    keep_mask = (seg_group == first_label[:, None]) & alive_group
    factor = jnp.where(keep_mask[:, None, :], jnp.exp(cum_group - before[:, :, None]), 0.0)
    weighted = (factor.transpose(0, 2, 1)[:, :, :, None] * grad_group).astype(jnp.bfloat16)
    states = jnp.einsum("clhp,cln->chpn", weighted, query_group, preferred_element_type=jnp.float32)
    group_gains = jnp.exp(cum_group[:, :, -1] - before)
    joined = (first_label == last_label).astype(jnp.float32)
    linked = jnp.concatenate(
        [jnp.ones((1,), jnp.float32), (last_label[:-1] == first_label[1:]).astype(jnp.float32)]
    )

    flow = joined[:, None] * group_gains * jnp.concatenate(
        [linked[1:], jnp.zeros((1,), jnp.float32)]
    )[:, None]
    carry_at = jnp.arange(groups + 1)[:, None, None]
    state_at = jnp.arange(groups)[None, :, None]
    step_at = jnp.arange(groups)[None, None, :]
    inside = (carry_at <= step_at) & (step_at < state_at)
    spans = jnp.prod(jnp.where(inside[None], flow.T[:, None, None, :], 1.0), axis=3)
    link_at = jnp.concatenate([linked, jnp.zeros((1,), jnp.float32)])
    coef = jnp.where((carry_at[:, :, 0] <= state_at[:, :, 0])[None], spans, 0.0) * link_at[None, :, None]
    carries = jnp.einsum(
        "hcd,dhpn->chpn", coef, states, precision=lax.Precision.HIGHEST
    )
    start_grad = carries[0]
    end_grads = carries[1:]
    return (
        cum_sums,
        cum_group,
        seg_group,
        alive_group,
        last_label,
        grad_group,
        end_grads,
        start_grad,
    )


def group_output(key_rows, queries, parts):
    cum_sums, cum_group, seg_group, alive_group, last_label, grad_group, end_grads, start_grad = (
        parts
    )
    groups = seg_group.shape[0]
    head_count = cum_group.shape[1]
    key_group = key_rows.reshape(groups, GROUP, N)
    query_group = queries.reshape(groups, GROUP, N)
    scores = jnp.einsum("csn,ctn->cst", query_group, key_group, preferred_element_type=jnp.float32)
    row_index = lax.broadcasted_iota(jnp.int32, (GROUP, GROUP), 0)
    col_index = lax.broadcasted_iota(jnp.int32, (GROUP, GROUP), 1)
    keep_mask = (
        (row_index >= col_index)[None]
        & (seg_group[:, :, None] == seg_group[:, None, :])
        & alive_group[:, :, None]
    )
    spread = cum_group[:, :, :, None] - cum_group[:, :, None, :]
    decays = jnp.exp(jnp.where(keep_mask[:, None], spread, -jnp.inf))
    mixing = (scores[:, None] * decays).astype(jnp.bfloat16)
    inner_part = jnp.einsum(
        "chst,cshp->cthp", mixing, grad_group, preferred_element_type=jnp.float32
    )
    across = jnp.einsum(
        "chpn,ctn->cthp",
        end_grads.astype(jnp.bfloat16),
        key_group,
        preferred_element_type=jnp.float32,
    )
    reach_weight = jnp.where(
        (seg_group == last_label[:, None])[:, None, :],
        jnp.exp(cum_group[:, :, -1:] - cum_group),
        0.0,
    )
    summed_parts = inner_part + across * reach_weight.transpose(0, 2, 1)[:, :, :, None]
    return summed_parts.reshape(groups * GROUP, head_count * P_SIZE)


def initial_state(out_grad, queries, decay, segment, alive_mask, cum_sums):
    tokens = out_grad.shape[0]
    head_count = decay.shape[0]
    firsts = jnp.concatenate([jnp.ones((1,), jnp.bool_), segment[1:] != segment[:-1]])
    labels = jnp.arange(RESP_DEV + 1, dtype=jnp.int32)
    member = segment[:, None] == labels[None, :]
    opening = cum_sums - decay
    base_label = jnp.sum(
        jnp.where((member & firsts[:, None])[None], opening[:, :, None], 0.0), axis=1
    )
    base_token = jnp.sum(jnp.where(member[None], base_label[:, None, :], 0.0), axis=2)
    factor = jnp.where(alive_mask[None], jnp.exp(cum_sums - base_token), 0.0)
    weighted = (factor.T[:, :, None] * out_grad.reshape(tokens, head_count, P_SIZE)).astype(
        jnp.bfloat16
    )
    return jnp.einsum("thp,tn->hpn", weighted, queries, preferred_element_type=jnp.float32)


def on_device(
    prompt_grad,
    prompt_keys,
    prompt_queries,
    prompt_decay,
    resp_grad,
    resp_keys,
    resp_queries,
    resp_decay,
    resp_segment,
):
    resp_alive = resp_segment < RESP_DEV
    resp_parts = group_parts(resp_grad, resp_queries, resp_decay, resp_segment, resp_alive)
    resp_dx = group_output(resp_keys, resp_queries, resp_parts).astype(jnp.bfloat16)
    partial_state = initial_state(
        resp_grad, resp_queries, resp_decay, resp_segment, resp_alive, resp_parts[0]
    )
    resp_len = lax.axis_size("resp")
    head_count = prompt_decay.shape[0]
    prompt_len = prompt_grad.shape[0]
    zero_label = jnp.zeros((prompt_len,), jnp.int32)
    all_alive = jnp.ones((prompt_len,), jnp.bool_)
    prompt_parts = group_parts(prompt_grad, prompt_queries, prompt_decay, zero_label, all_alive)
    cum_sums = prompt_parts[0]
    start_grad = prompt_parts[7]
    shard_total = cum_sums[:, -1]
    seq_index = lax.axis_index("seq")
    seq_len = lax.axis_size("seq")
    share = head_count // partial_state.shape[0]
    pieces = []
    for turn in range(share):
        pairs = []
        for src_seq in range(seq_len):
            for src_resp in range(resp_len):
                dst_seq = share * src_resp + (src_seq % share + turn) % share
                dst_resp = src_seq // share
                pairs.append((src_seq * resp_len + src_resp, dst_seq * resp_len + dst_resp))
        pieces.append(lax.ppermute(partial_state, ("seq", "resp"), pairs))
    pieces = jnp.stack(pieces)
    order = (seq_index % share - jnp.arange(share)) % share
    my_heads = jnp.take(pieces, order, axis=0).reshape((head_count,) + partial_state.shape[1:])
    own_a = jnp.exp(shard_total)
    whole_b = start_grad
    whole_a = own_a
    later_b = jnp.zeros_like(start_grad)
    later_a = jnp.ones_like(own_a)
    span = 1
    while span < seq_len:
        radix = min(4, seq_len // span)
        parts = [whole_b, jnp.broadcast_to(whole_a[:, None, None], (head_count, 1, N))]
        if span >= share:
            parts.append(my_heads)
        message = jnp.concatenate(parts, axis=1)
        gots = []
        for step in range(1, radix):
            shift = span * step
            pairs = [((k + shift) % seq_len, k) for k in range(seq_len)]
            gots.append((shift, lax.ppermute(message, "seq", pairs)))
        summed_heads = my_heads
        for shift, got in gots:
            valid = seq_index + shift < seq_len
            got_b = jnp.where(valid, got[:, :P_SIZE], 0.0)
            got_a = jnp.where(valid, got[:, P_SIZE, 0], 1.0)
            later_b = later_b + later_a[:, None, None] * got_b
            later_a = later_a * got_a
            if span >= share:
                summed_heads = summed_heads + got[:, P_SIZE + 1 :]
        my_heads = summed_heads
        whole_b = start_grad + own_a[:, None, None] * later_b
        whole_a = own_a * later_a
        span *= radix
    incoming = later_b + later_a[:, None, None] * my_heads
    local_part = group_output(prompt_keys, prompt_queries, prompt_parts)
    carry_term = jnp.einsum(
        "hpn,tn->thp",
        incoming.astype(jnp.bfloat16),
        prompt_keys,
        preferred_element_type=jnp.float32,
    )
    carry_term = carry_term * jnp.exp(shard_total[:, None] - cum_sums).T[:, :, None]
    prompt_dx = (local_part + carry_term.reshape(prompt_len, head_count * P_SIZE)).astype(
        jnp.bfloat16
    )
    return (prompt_dx, resp_dx)


def solution(mesh):
    return jax.shard_map(
        on_device,
        mesh=mesh,
        in_specs=(
            P("seq", "resp"),
            P("seq", None),
            P("seq", None),
            P("resp", "seq"),
            P("resp", "seq"),
            P("resp", None),
            P("resp", None),
            P("seq", "resp"),
            P("resp"),
        ),
        out_specs=(P("seq", "resp"), P("resp", "seq")),
        check_vma=False,
    )
```

```python
import jax
import jax.numpy as jnp
from jax import lax
from jax.sharding import PartitionSpec as P

P_SIZE = 64
N = 128
GROUP = 256
RESP_DEV = 8


def group_parts(out_grad, queries, decay, segment, alive_mask):
    tokens = out_grad.shape[0]
    head_count = decay.shape[0]
    groups = tokens // GROUP
    cum_sums = jnp.cumsum(decay, axis=1)
    cum_group = cum_sums.reshape(head_count, groups, GROUP).transpose(1, 0, 2)
    decay_group = decay.reshape(head_count, groups, GROUP).transpose(1, 0, 2)
    before = cum_group[:, :, 0] - decay_group[:, :, 0]
    seg_group = segment.reshape(groups, GROUP)
    alive_group = alive_mask.reshape(groups, GROUP)
    first_label = seg_group[:, 0]
    last_label = seg_group[:, -1]
    grad_group = out_grad.reshape(groups, GROUP, head_count, P_SIZE)
    query_group = queries.reshape(groups, GROUP, N)
    keep_mask = (seg_group == first_label[:, None]) & alive_group
    factor = jnp.where(keep_mask[:, None, :], jnp.exp(cum_group - before[:, :, None]), 0.0)
    weighted = (factor.transpose(0, 2, 1)[:, :, :, None] * grad_group).astype(jnp.bfloat16)
    states = jnp.einsum("clhp,cln->chpn", weighted, query_group, preferred_element_type=jnp.float32)
    group_gains = jnp.exp(cum_group[:, :, -1] - before)
    joined = (first_label == last_label).astype(jnp.float32)
    linked = jnp.concatenate(
        [jnp.ones((1,), jnp.float32), (last_label[:-1] == first_label[1:]).astype(jnp.float32)]
    )

    flow = joined[:, None] * group_gains * jnp.concatenate(
        [linked[1:], jnp.zeros((1,), jnp.float32)]
    )[:, None]
    carry_at = jnp.arange(groups + 1)[:, None, None]
    state_at = jnp.arange(groups)[None, :, None]
    step_at = jnp.arange(groups)[None, None, :]
    inside = (carry_at <= step_at) & (step_at < state_at)
    spans = jnp.prod(jnp.where(inside[None], flow.T[:, None, None, :], 1.0), axis=3)
    link_at = jnp.concatenate([linked, jnp.zeros((1,), jnp.float32)])
    coef = jnp.where((carry_at[:, :, 0] <= state_at[:, :, 0])[None], spans, 0.0) * link_at[None, :, None]
    carries = jnp.einsum(
        "hcd,dhpn->chpn", coef, states, precision=lax.Precision.HIGHEST
    )
    start_grad = carries[0]
    end_grads = carries[1:]
    return (
        cum_sums,
        cum_group,
        seg_group,
        alive_group,
        last_label,
        grad_group,
        end_grads,
        start_grad,
    )


def group_output(key_rows, queries, parts):
    cum_sums, cum_group, seg_group, alive_group, last_label, grad_group, end_grads, start_grad = (
        parts
    )
    groups = seg_group.shape[0]
    head_count = cum_group.shape[1]
    key_group = key_rows.reshape(groups, GROUP, N)
    query_group = queries.reshape(groups, GROUP, N)
    scores = jnp.einsum("csn,ctn->cst", query_group, key_group, preferred_element_type=jnp.float32)
    row_index = lax.broadcasted_iota(jnp.int32, (GROUP, GROUP), 0)
    col_index = lax.broadcasted_iota(jnp.int32, (GROUP, GROUP), 1)
    keep_mask = (
        (row_index >= col_index)[None]
        & (seg_group[:, :, None] == seg_group[:, None, :])
        & alive_group[:, :, None]
    )
    spread = cum_group[:, :, :, None] - cum_group[:, :, None, :]
    decays = jnp.exp(jnp.where(keep_mask[:, None], spread, -jnp.inf))
    mixing = (scores[:, None] * decays).astype(jnp.bfloat16)
    inner_part = jnp.einsum(
        "chst,cshp->cthp", mixing, grad_group, preferred_element_type=jnp.float32
    )
    across = jnp.einsum(
        "chpn,ctn->cthp",
        end_grads.astype(jnp.bfloat16),
        key_group,
        preferred_element_type=jnp.float32,
    )
    reach_weight = jnp.where(
        (seg_group == last_label[:, None])[:, None, :],
        jnp.exp(cum_group[:, :, -1:] - cum_group),
        0.0,
    )
    summed_parts = inner_part + across * reach_weight.transpose(0, 2, 1)[:, :, :, None]
    return summed_parts.reshape(groups * GROUP, head_count * P_SIZE)


def initial_state(out_grad, queries, decay, segment, alive_mask, cum_sums):
    tokens = out_grad.shape[0]
    head_count = decay.shape[0]
    firsts = jnp.concatenate([jnp.ones((1,), jnp.bool_), segment[1:] != segment[:-1]])
    labels = jnp.arange(RESP_DEV + 1, dtype=jnp.int32)
    member = segment[:, None] == labels[None, :]
    opening = cum_sums - decay
    base_label = jnp.sum(
        jnp.where((member & firsts[:, None])[None], opening[:, :, None], 0.0), axis=1
    )
    base_token = jnp.sum(jnp.where(member[None], base_label[:, None, :], 0.0), axis=2)
    factor = jnp.where(alive_mask[None], jnp.exp(cum_sums - base_token), 0.0)
    weighted = (factor.T[:, :, None] * out_grad.reshape(tokens, head_count, P_SIZE)).astype(
        jnp.bfloat16
    )
    return jnp.einsum("thp,tn->hpn", weighted, queries, preferred_element_type=jnp.float32)


def on_device(
    prompt_grad,
    prompt_keys,
    prompt_queries,
    prompt_decay,
    resp_grad,
    resp_keys,
    resp_queries,
    resp_decay,
    resp_segment,
):
    resp_alive = resp_segment < RESP_DEV
    resp_parts = group_parts(resp_grad, resp_queries, resp_decay, resp_segment, resp_alive)
    resp_dx = group_output(resp_keys, resp_queries, resp_parts).astype(jnp.bfloat16)
    partial_state = initial_state(
        resp_grad, resp_queries, resp_decay, resp_segment, resp_alive, resp_parts[0]
    )
    resp_len = lax.axis_size("resp")
    head_count = prompt_decay.shape[0]
    prompt_len = prompt_grad.shape[0]
    zero_label = jnp.zeros((prompt_len,), jnp.int32)
    all_alive = jnp.ones((prompt_len,), jnp.bool_)
    prompt_parts = group_parts(prompt_grad, prompt_queries, prompt_decay, zero_label, all_alive)
    cum_sums = prompt_parts[0]
    start_grad = prompt_parts[7]
    shard_total = cum_sums[:, -1]
    seq_index = lax.axis_index("seq")
    seq_len = lax.axis_size("seq")
    share = head_count // partial_state.shape[0]
    pairs = []
    for src_seq in range(seq_len):
        for src_resp in range(resp_len):
            dst_seq = share * src_resp + src_seq % share
            dst_resp = src_seq // share
            pairs.append((src_seq * resp_len + src_resp, dst_seq * resp_len + dst_resp))
    pieces = lax.ppermute(partial_state, ("seq", "resp"), pairs)[None]
    whole_b = start_grad
    whole_a = jnp.exp(shard_total)
    later_b = jnp.zeros_like(start_grad)
    later_a = jnp.ones_like(whole_a)
    my_heads = None
    shift = 1
    while shift < seq_len:
        pairs = [((k + shift) % seq_len, k) for k in range(seq_len)]
        parts = [whole_b, jnp.broadcast_to(whole_a[:, None, None], (head_count, 1, N))]
        if my_heads is None:
            parts.append(pieces.reshape(head_count, -1, N))
        else:
            parts.append(my_heads)
        got = lax.ppermute(jnp.concatenate(parts, axis=1), "seq", pairs)
        valid = seq_index + shift < seq_len
        got_b = jnp.where(valid, got[:, :P_SIZE], 0.0)
        got_a = jnp.where(valid, got[:, P_SIZE, 0], 1.0)
        rest = got[:, P_SIZE + 1 :]
        if my_heads is None:
            pieces = jnp.concatenate([pieces, rest.reshape(pieces.shape)], axis=0)
            if pieces.shape[0] == share:
                order = (jnp.arange(share) - seq_index % share) % share
                my_heads = jnp.take(pieces, order, axis=0).reshape(
                    (head_count,) + partial_state.shape[1:]
                )
        else:
            my_heads = my_heads + rest
        later_b = later_b + later_a[:, None, None] * got_b
        later_a = later_a * got_a
        if shift * 2 < seq_len:
            whole_b = whole_b + whole_a[:, None, None] * got_b
            whole_a = whole_a * got_a
        shift *= 2
    incoming = later_b + later_a[:, None, None] * my_heads
    local_part = group_output(prompt_keys, prompt_queries, prompt_parts)
    carry_term = jnp.einsum(
        "hpn,tn->thp",
        incoming.astype(jnp.bfloat16),
        prompt_keys,
        preferred_element_type=jnp.float32,
    )
    carry_term = carry_term * jnp.exp(shard_total[:, None] - cum_sums).T[:, :, None]
    prompt_dx = (local_part + carry_term.reshape(prompt_len, head_count * P_SIZE)).astype(
        jnp.bfloat16
    )
    return (prompt_dx, resp_dx)


def solution(mesh):
    return jax.shard_map(
        on_device,
        mesh=mesh,
        in_specs=(
            P("seq", "resp"),
            P("seq", None),
            P("seq", None),
            P("resp", "seq"),
            P("resp", "seq"),
            P("resp", None),
            P("resp", None),
            P("seq", "resp"),
            P("resp"),
        ),
        out_specs=(P("seq", "resp"), P("resp", "seq")),
        check_vma=False,
    )
```

```python
import jax
import jax.numpy as jnp
from jax import lax
from jax.sharding import PartitionSpec as P

P_SIZE = 64
N = 128
GROUP = 256
RESP_DEV = 8


def group_parts(out_grad, queries, decay, segment, alive_mask):
    tokens = out_grad.shape[0]
    head_count = decay.shape[0]
    groups = tokens // GROUP
    cum_sums = jnp.cumsum(decay, axis=1)
    cum_group = cum_sums.reshape(head_count, groups, GROUP).transpose(1, 0, 2)
    decay_group = decay.reshape(head_count, groups, GROUP).transpose(1, 0, 2)
    before = cum_group[:, :, 0] - decay_group[:, :, 0]
    seg_group = segment.reshape(groups, GROUP)
    alive_group = alive_mask.reshape(groups, GROUP)
    first_label = seg_group[:, 0]
    last_label = seg_group[:, -1]
    grad_group = out_grad.reshape(groups, GROUP, head_count, P_SIZE)
    query_group = queries.reshape(groups, GROUP, N)
    keep_mask = (seg_group == first_label[:, None]) & alive_group
    factor = jnp.where(keep_mask[:, None, :], jnp.exp(cum_group - before[:, :, None]), 0.0)
    weighted = (factor.transpose(0, 2, 1)[:, :, :, None] * grad_group).astype(jnp.bfloat16)
    states = jnp.einsum("clhp,cln->chpn", weighted, query_group, preferred_element_type=jnp.float32)
    group_gains = jnp.exp(cum_group[:, :, -1] - before)
    joined = (first_label == last_label).astype(jnp.float32)
    linked = jnp.concatenate(
        [jnp.ones((1,), jnp.float32), (last_label[:-1] == first_label[1:]).astype(jnp.float32)]
    )

    flow = joined[:, None] * group_gains * jnp.concatenate(
        [linked[1:], jnp.zeros((1,), jnp.float32)]
    )[:, None]
    carry_at = jnp.arange(groups + 1)[:, None, None]
    state_at = jnp.arange(groups)[None, :, None]
    step_at = jnp.arange(groups)[None, None, :]
    inside = (carry_at <= step_at) & (step_at < state_at)
    spans = jnp.prod(jnp.where(inside[None], flow.T[:, None, None, :], 1.0), axis=3)
    link_at = jnp.concatenate([linked, jnp.zeros((1,), jnp.float32)])
    coef = jnp.where((carry_at[:, :, 0] <= state_at[:, :, 0])[None], spans, 0.0) * link_at[None, :, None]
    carries = jnp.einsum(
        "hcd,dhpn->chpn", coef, states, precision=lax.Precision.HIGHEST
    )
    start_grad = carries[0]
    end_grads = carries[1:]
    return (
        cum_sums,
        cum_group,
        seg_group,
        alive_group,
        last_label,
        grad_group,
        end_grads,
        start_grad,
    )


def group_output(key_rows, queries, parts):
    cum_sums, cum_group, seg_group, alive_group, last_label, grad_group, end_grads, start_grad = (
        parts
    )
    groups = seg_group.shape[0]
    head_count = cum_group.shape[1]
    key_group = key_rows.reshape(groups, GROUP, N)
    query_group = queries.reshape(groups, GROUP, N)
    scores = jnp.einsum("csn,ctn->cst", query_group, key_group, preferred_element_type=jnp.float32)
    row_index = lax.broadcasted_iota(jnp.int32, (GROUP, GROUP), 0)
    col_index = lax.broadcasted_iota(jnp.int32, (GROUP, GROUP), 1)
    keep_mask = (
        (row_index >= col_index)[None]
        & (seg_group[:, :, None] == seg_group[:, None, :])
        & alive_group[:, :, None]
    )
    spread = cum_group[:, :, :, None] - cum_group[:, :, None, :]
    decays = jnp.exp(jnp.where(keep_mask[:, None], spread, -jnp.inf))
    mixing = (scores[:, None] * decays).astype(jnp.bfloat16)
    inner_part = jnp.einsum(
        "chst,cshp->cthp", mixing, grad_group, preferred_element_type=jnp.float32
    )
    across = jnp.einsum(
        "chpn,ctn->cthp",
        end_grads.astype(jnp.bfloat16),
        key_group,
        preferred_element_type=jnp.float32,
    )
    reach_weight = jnp.where(
        (seg_group == last_label[:, None])[:, None, :],
        jnp.exp(cum_group[:, :, -1:] - cum_group),
        0.0,
    )
    summed_parts = inner_part + across * reach_weight.transpose(0, 2, 1)[:, :, :, None]
    return summed_parts.reshape(groups * GROUP, head_count * P_SIZE)


def initial_state(out_grad, queries, decay, segment, alive_mask, cum_sums):
    tokens = out_grad.shape[0]
    head_count = decay.shape[0]
    firsts = jnp.concatenate([jnp.ones((1,), jnp.bool_), segment[1:] != segment[:-1]])
    labels = jnp.arange(RESP_DEV + 1, dtype=jnp.int32)
    member = segment[:, None] == labels[None, :]
    opening = cum_sums - decay
    base_label = jnp.sum(
        jnp.where((member & firsts[:, None])[None], opening[:, :, None], 0.0), axis=1
    )
    base_token = jnp.sum(jnp.where(member[None], base_label[:, None, :], 0.0), axis=2)
    factor = jnp.where(alive_mask[None], jnp.exp(cum_sums - base_token), 0.0)
    weighted = (factor.T[:, :, None] * out_grad.reshape(tokens, head_count, P_SIZE)).astype(
        jnp.bfloat16
    )
    return jnp.einsum("thp,tn->hpn", weighted, queries, preferred_element_type=jnp.float32)


def on_device(
    prompt_grad,
    prompt_keys,
    prompt_queries,
    prompt_decay,
    resp_grad,
    resp_keys,
    resp_queries,
    resp_decay,
    resp_segment,
):
    resp_alive = resp_segment < RESP_DEV
    resp_parts = group_parts(resp_grad, resp_queries, resp_decay, resp_segment, resp_alive)
    resp_dx = group_output(resp_keys, resp_queries, resp_parts).astype(jnp.bfloat16)
    partial_state = initial_state(
        resp_grad, resp_queries, resp_decay, resp_segment, resp_alive, resp_parts[0]
    )
    resp_len = lax.axis_size("resp")
    head_count = prompt_decay.shape[0]
    prompt_len = prompt_grad.shape[0]
    zero_label = jnp.zeros((prompt_len,), jnp.int32)
    all_alive = jnp.ones((prompt_len,), jnp.bool_)
    prompt_parts = group_parts(prompt_grad, prompt_queries, prompt_decay, zero_label, all_alive)
    cum_sums = prompt_parts[0]
    start_grad = prompt_parts[7]
    shard_total = cum_sums[:, -1]
    seq_index = lax.axis_index("seq")
    seq_len = lax.axis_size("seq")
    share = head_count // partial_state.shape[0]
    pairs = []
    for src_seq in range(seq_len):
        for src_resp in range(resp_len):
            dst_seq = share * src_resp + src_seq % share
            dst_resp = src_seq // share
            pairs.append((src_seq * resp_len + src_resp, dst_seq * resp_len + dst_resp))
    partial_state, cum_sums = lax.optimization_barrier((partial_state, cum_sums))
    pieces = lax.ppermute(partial_state, ("seq", "resp"), pairs)[None]
    whole_b = start_grad
    whole_a = jnp.exp(shard_total)
    later_b = jnp.zeros_like(start_grad)
    later_a = jnp.ones_like(whole_a)
    my_heads = None
    shift = 1
    while shift < seq_len:
        pairs = [((k + shift) % seq_len, k) for k in range(seq_len)]
        parts = [whole_b, jnp.broadcast_to(whole_a[:, None, None], (head_count, 1, N))]
        if my_heads is None:
            parts.append(pieces.reshape(head_count, -1, N))
        else:
            parts.append(my_heads)
        got = lax.ppermute(jnp.concatenate(parts, axis=1), "seq", pairs)
        valid = seq_index + shift < seq_len
        got_b = jnp.where(valid, got[:, :P_SIZE], 0.0)
        got_a = jnp.where(valid, got[:, P_SIZE, 0], 1.0)
        rest = got[:, P_SIZE + 1 :]
        if my_heads is None:
            pieces = jnp.concatenate([pieces, rest.reshape(pieces.shape)], axis=0)
            if pieces.shape[0] == share:
                order = (jnp.arange(share) - seq_index % share) % share
                my_heads = jnp.take(pieces, order, axis=0).reshape(
                    (head_count,) + partial_state.shape[1:]
                )
        else:
            my_heads = my_heads + rest
        later_b = later_b + later_a[:, None, None] * got_b
        later_a = later_a * got_a
        if shift * 2 < seq_len:
            whole_b = whole_b + whole_a[:, None, None] * got_b
            whole_a = whole_a * got_a
        shift *= 2
    incoming = later_b + later_a[:, None, None] * my_heads
    local_part = group_output(prompt_keys, prompt_queries, prompt_parts)
    carry_term = jnp.einsum(
        "hpn,tn->thp",
        incoming.astype(jnp.bfloat16),
        prompt_keys,
        preferred_element_type=jnp.float32,
    )
    carry_term = carry_term * jnp.exp(shard_total[:, None] - cum_sums).T[:, :, None]
    prompt_dx = (local_part + carry_term.reshape(prompt_len, head_count * P_SIZE)).astype(
        jnp.bfloat16
    )
    return (prompt_dx, resp_dx)


def solution(mesh):
    return jax.shard_map(
        on_device,
        mesh=mesh,
        in_specs=(
            P("seq", "resp"),
            P("seq", None),
            P("seq", None),
            P("resp", "seq"),
            P("resp", "seq"),
            P("resp", None),
            P("resp", None),
            P("seq", "resp"),
            P("resp"),
        ),
        out_specs=(P("seq", "resp"), P("resp", "seq")),
        check_vma=False,
    )
```

```python
import jax
import jax.numpy as jnp
from jax import lax
from jax.sharding import PartitionSpec as P

P_SIZE = 64
N = 128
GROUP = 256
RESP_DEV = 8


def group_parts(out_grad, queries, decay, segment, alive_mask):
    tokens = out_grad.shape[0]
    head_count = decay.shape[0]
    groups = tokens // GROUP
    cum_sums = jnp.cumsum(decay, axis=1)
    cum_group = cum_sums.reshape(head_count, groups, GROUP).transpose(1, 0, 2)
    decay_group = decay.reshape(head_count, groups, GROUP).transpose(1, 0, 2)
    before = cum_group[:, :, 0] - decay_group[:, :, 0]
    seg_group = segment.reshape(groups, GROUP)
    alive_group = alive_mask.reshape(groups, GROUP)
    first_label = seg_group[:, 0]
    last_label = seg_group[:, -1]
    grad_group = out_grad.reshape(groups, GROUP, head_count, P_SIZE)
    query_group = queries.reshape(groups, GROUP, N)
    keep_mask = (seg_group == first_label[:, None]) & alive_group
    factor = jnp.where(keep_mask[:, None, :], jnp.exp(cum_group - before[:, :, None]), 0.0)
    weighted = (factor.transpose(0, 2, 1)[:, :, :, None] * grad_group).astype(jnp.bfloat16)
    states = jnp.einsum("clhp,cln->chpn", weighted, query_group, preferred_element_type=jnp.float32)
    group_gains = jnp.exp(cum_group[:, :, -1] - before)
    joined = (first_label == last_label).astype(jnp.float32)
    linked = jnp.concatenate(
        [jnp.ones((1,), jnp.float32), (last_label[:-1] == first_label[1:]).astype(jnp.float32)]
    )

    flow = joined[:, None] * group_gains * jnp.concatenate(
        [linked[1:], jnp.zeros((1,), jnp.float32)]
    )[:, None]
    carry_at = jnp.arange(groups + 1)[:, None, None]
    state_at = jnp.arange(groups)[None, :, None]
    step_at = jnp.arange(groups)[None, None, :]
    inside = (carry_at <= step_at) & (step_at < state_at)
    spans = jnp.prod(jnp.where(inside[None], flow.T[:, None, None, :], 1.0), axis=3)
    link_at = jnp.concatenate([linked, jnp.zeros((1,), jnp.float32)])
    coef = jnp.where((carry_at[:, :, 0] <= state_at[:, :, 0])[None], spans, 0.0) * link_at[None, :, None]
    carries = jnp.einsum(
        "hcd,dhpn->chpn", coef, states, precision=lax.Precision.HIGHEST
    )
    start_grad = carries[0]
    end_grads = carries[1:]
    return (
        cum_sums,
        cum_group,
        seg_group,
        alive_group,
        last_label,
        grad_group,
        end_grads,
        start_grad,
    )


def group_output(key_rows, queries, parts):
    cum_sums, cum_group, seg_group, alive_group, last_label, grad_group, end_grads, start_grad = (
        parts
    )
    groups = seg_group.shape[0]
    head_count = cum_group.shape[1]
    key_group = key_rows.reshape(groups, GROUP, N)
    query_group = queries.reshape(groups, GROUP, N)
    scores = jnp.einsum("csn,ctn->cst", query_group, key_group, preferred_element_type=jnp.float32)
    row_index = lax.broadcasted_iota(jnp.int32, (GROUP, GROUP), 0)
    col_index = lax.broadcasted_iota(jnp.int32, (GROUP, GROUP), 1)
    keep_mask = (
        (row_index >= col_index)[None]
        & (seg_group[:, :, None] == seg_group[:, None, :])
        & alive_group[:, :, None]
    )
    spread = cum_group[:, :, :, None] - cum_group[:, :, None, :]
    decays = jnp.exp(jnp.where(keep_mask[:, None], spread, -jnp.inf))
    mixing = (scores[:, None] * decays).astype(jnp.bfloat16)
    inner_part = jnp.einsum(
        "chst,cshp->cthp", mixing, grad_group, preferred_element_type=jnp.float32
    )
    across = jnp.einsum(
        "chpn,ctn->cthp",
        end_grads.astype(jnp.bfloat16),
        key_group,
        preferred_element_type=jnp.float32,
    )
    reach_weight = jnp.where(
        (seg_group == last_label[:, None])[:, None, :],
        jnp.exp(cum_group[:, :, -1:] - cum_group),
        0.0,
    )
    summed_parts = inner_part + across * reach_weight.transpose(0, 2, 1)[:, :, :, None]
    return summed_parts.reshape(groups * GROUP, head_count * P_SIZE)


def initial_state(out_grad, queries, decay, segment, alive_mask, cum_sums):
    tokens = out_grad.shape[0]
    head_count = decay.shape[0]
    firsts = jnp.concatenate([jnp.ones((1,), jnp.bool_), segment[1:] != segment[:-1]])
    labels = jnp.arange(RESP_DEV + 1, dtype=jnp.int32)
    member = segment[:, None] == labels[None, :]
    opening = cum_sums - decay
    base_label = jnp.sum(
        jnp.where((member & firsts[:, None])[None], opening[:, :, None], 0.0), axis=1
    )
    base_token = jnp.sum(jnp.where(member[None], base_label[:, None, :], 0.0), axis=2)
    factor = jnp.where(alive_mask[None], jnp.exp(cum_sums - base_token), 0.0)
    weighted = (factor.T[:, :, None] * out_grad.reshape(tokens, head_count, P_SIZE)).astype(
        jnp.bfloat16
    )
    return jnp.einsum("thp,tn->hpn", weighted, queries, preferred_element_type=jnp.float32)


def on_device(
    prompt_grad,
    prompt_keys,
    prompt_queries,
    prompt_decay,
    resp_grad,
    resp_keys,
    resp_queries,
    resp_decay,
    resp_segment,
):
    resp_alive = resp_segment < RESP_DEV
    partial_state = initial_state(
        resp_grad, resp_queries, resp_decay, resp_segment, resp_alive, jnp.cumsum(resp_decay, axis=1)
    )
    resp_len = lax.axis_size("resp")
    head_count = prompt_decay.shape[0]
    prompt_len = prompt_grad.shape[0]
    zero_label = jnp.zeros((prompt_len,), jnp.int32)
    all_alive = jnp.ones((prompt_len,), jnp.bool_)
    prompt_parts = group_parts(prompt_grad, prompt_queries, prompt_decay, zero_label, all_alive)
    cum_sums = prompt_parts[0]
    start_grad = prompt_parts[7]
    shard_total = cum_sums[:, -1]
    seq_index = lax.axis_index("seq")
    seq_len = lax.axis_size("seq")
    share = head_count // partial_state.shape[0]
    pairs = []
    for src_seq in range(seq_len):
        for src_resp in range(resp_len):
            dst_seq = share * src_resp + src_seq % share
            dst_resp = src_seq // share
            pairs.append((src_seq * resp_len + src_resp, dst_seq * resp_len + dst_resp))
    pieces = lax.ppermute(partial_state, ("seq", "resp"), pairs)[None]
    whole_b = start_grad
    whole_a = jnp.exp(shard_total)
    later_b = jnp.zeros_like(start_grad)
    later_a = jnp.ones_like(whole_a)
    my_heads = None
    shift = 1
    while shift < seq_len:
        pairs = [((k + shift) % seq_len, k) for k in range(seq_len)]
        parts = [whole_b, jnp.broadcast_to(whole_a[:, None, None], (head_count, 1, N))]
        if my_heads is None:
            parts.append(pieces.reshape(head_count, -1, N))
        else:
            parts.append(my_heads)
        message = jnp.concatenate(parts, axis=1)
        if shift == 1:
            message, resp_grad, resp_keys, prompt_keys, prompt_parts = lax.optimization_barrier(
                (message, resp_grad, resp_keys, prompt_keys, prompt_parts)
            )
        got = lax.ppermute(message, "seq", pairs)
        valid = seq_index + shift < seq_len
        got_b = jnp.where(valid, got[:, :P_SIZE], 0.0)
        got_a = jnp.where(valid, got[:, P_SIZE, 0], 1.0)
        rest = got[:, P_SIZE + 1 :]
        if my_heads is None:
            pieces = jnp.concatenate([pieces, rest.reshape(pieces.shape)], axis=0)
            if pieces.shape[0] == share:
                order = (jnp.arange(share) - seq_index % share) % share
                my_heads = jnp.take(pieces, order, axis=0).reshape(
                    (head_count,) + partial_state.shape[1:]
                )
        else:
            my_heads = my_heads + rest
        later_b = later_b + later_a[:, None, None] * got_b
        later_a = later_a * got_a
        if shift * 2 < seq_len:
            whole_b = whole_b + whole_a[:, None, None] * got_b
            whole_a = whole_a * got_a
        shift *= 2
    incoming = later_b + later_a[:, None, None] * my_heads
    resp_parts = group_parts(resp_grad, resp_queries, resp_decay, resp_segment, resp_alive)
    resp_dx = group_output(resp_keys, resp_queries, resp_parts).astype(jnp.bfloat16)
    local_part = group_output(prompt_keys, prompt_queries, prompt_parts)
    cum_sums = prompt_parts[0]
    carry_term = jnp.einsum(
        "hpn,tn->thp",
        incoming.astype(jnp.bfloat16),
        prompt_keys,
        preferred_element_type=jnp.float32,
    )
    carry_term = carry_term * jnp.exp(shard_total[:, None] - cum_sums).T[:, :, None]
    prompt_dx = (local_part + carry_term.reshape(prompt_len, head_count * P_SIZE)).astype(
        jnp.bfloat16
    )
    return (prompt_dx, resp_dx)


def solution(mesh):
    return jax.shard_map(
        on_device,
        mesh=mesh,
        in_specs=(
            P("seq", "resp"),
            P("seq", None),
            P("seq", None),
            P("resp", "seq"),
            P("resp", "seq"),
            P("resp", None),
            P("resp", None),
            P("seq", "resp"),
            P("resp"),
        ),
        out_specs=(P("seq", "resp"), P("resp", "seq")),
        check_vma=False,
    )
```

```python
import jax
import jax.numpy as jnp
from jax import lax
from jax.experimental import pallas as pl
from jax.sharding import PartitionSpec as P

_INTERPRET = False

P_SIZE = 64
N = 128
GROUP = 256
RESP_DEV = 8


def group_parts(out_grad, queries, decay, segment, alive_mask):
    tokens = out_grad.shape[0]
    head_count = decay.shape[0]
    groups = tokens // GROUP
    cum_sums = jnp.cumsum(decay, axis=1)
    cum_group = cum_sums.reshape(head_count, groups, GROUP).transpose(1, 0, 2)
    decay_group = decay.reshape(head_count, groups, GROUP).transpose(1, 0, 2)
    before = cum_group[:, :, 0] - decay_group[:, :, 0]
    seg_group = segment.reshape(groups, GROUP)
    alive_group = alive_mask.reshape(groups, GROUP)
    first_label = seg_group[:, 0]
    last_label = seg_group[:, -1]
    grad_group = out_grad.reshape(groups, GROUP, head_count, P_SIZE)
    query_group = queries.reshape(groups, GROUP, N)
    keep_mask = (seg_group == first_label[:, None]) & alive_group
    factor = jnp.where(keep_mask[:, None, :], jnp.exp(cum_group - before[:, :, None]), 0.0)
    weighted = (factor.transpose(0, 2, 1)[:, :, :, None] * grad_group).astype(jnp.bfloat16)
    states = jnp.einsum("clhp,cln->chpn", weighted, query_group, preferred_element_type=jnp.float32)
    group_gains = jnp.exp(cum_group[:, :, -1] - before)
    joined = (first_label == last_label).astype(jnp.float32)
    linked = jnp.concatenate(
        [jnp.ones((1,), jnp.float32), (last_label[:-1] == first_label[1:]).astype(jnp.float32)]
    )

    flow = joined[:, None] * group_gains * jnp.concatenate(
        [linked[1:], jnp.zeros((1,), jnp.float32)]
    )[:, None]
    carry_at = jnp.arange(groups + 1)[:, None, None]
    state_at = jnp.arange(groups)[None, :, None]
    step_at = jnp.arange(groups)[None, None, :]
    inside = (carry_at <= step_at) & (step_at < state_at)
    spans = jnp.prod(jnp.where(inside[None], flow.T[:, None, None, :], 1.0), axis=3)
    link_at = jnp.concatenate([linked, jnp.zeros((1,), jnp.float32)])
    coef = jnp.where((carry_at[:, :, 0] <= state_at[:, :, 0])[None], spans, 0.0) * link_at[None, :, None]
    carries = jnp.einsum(
        "hcd,dhpn->chpn", coef, states, precision=lax.Precision.HIGHEST
    )
    start_grad = carries[0]
    end_grads = carries[1:]
    return (
        cum_sums,
        cum_group,
        seg_group,
        alive_group,
        last_label,
        grad_group,
        end_grads,
        start_grad,
    )


def group_output(key_rows, queries, parts):
    cum_sums, cum_group, seg_group, alive_group, last_label, grad_group, end_grads, start_grad = (
        parts
    )
    groups = seg_group.shape[0]
    head_count = cum_group.shape[1]
    key_group = key_rows.reshape(groups, GROUP, N)
    query_group = queries.reshape(groups, GROUP, N)
    scores = jnp.einsum("csn,ctn->cst", query_group, key_group, preferred_element_type=jnp.float32)
    row_index = lax.broadcasted_iota(jnp.int32, (GROUP, GROUP), 0)
    col_index = lax.broadcasted_iota(jnp.int32, (GROUP, GROUP), 1)
    keep_mask = (
        (row_index >= col_index)[None]
        & (seg_group[:, :, None] == seg_group[:, None, :])
        & alive_group[:, :, None]
    )
    spread = cum_group[:, :, :, None] - cum_group[:, :, None, :]
    decays = jnp.exp(jnp.where(keep_mask[:, None], spread, -jnp.inf))
    mixing = (scores[:, None] * decays).astype(jnp.bfloat16)
    inner_part = jnp.einsum(
        "chst,cshp->cthp", mixing, grad_group, preferred_element_type=jnp.float32
    )
    across = jnp.einsum(
        "chpn,ctn->cthp",
        end_grads.astype(jnp.bfloat16),
        key_group,
        preferred_element_type=jnp.float32,
    )
    reach_weight = jnp.where(
        (seg_group == last_label[:, None])[:, None, :],
        jnp.exp(cum_group[:, :, -1:] - cum_group),
        0.0,
    )
    summed_parts = inner_part + across * reach_weight.transpose(0, 2, 1)[:, :, :, None]
    return summed_parts.reshape(groups * GROUP, head_count * P_SIZE)


def initial_state(out_grad, queries, decay, segment, alive_mask, cum_sums):
    tokens = out_grad.shape[0]
    head_count = decay.shape[0]
    firsts = jnp.concatenate([jnp.ones((1,), jnp.bool_), segment[1:] != segment[:-1]])
    labels = jnp.arange(RESP_DEV + 1, dtype=jnp.int32)
    member = segment[:, None] == labels[None, :]
    opening = cum_sums - decay
    base_label = jnp.sum(
        jnp.where((member & firsts[:, None])[None], opening[:, :, None], 0.0), axis=1
    )
    base_token = jnp.sum(jnp.where(member[None], base_label[:, None, :], 0.0), axis=2)
    factor = jnp.where(alive_mask[None], jnp.exp(cum_sums - base_token), 0.0)
    weighted = (factor.T[:, :, None] * out_grad.reshape(tokens, head_count, P_SIZE)).astype(
        jnp.bfloat16
    )
    return jnp.einsum("thp,tn->hpn", weighted, queries, preferred_element_type=jnp.float32)


def _scan_round(flag_ref, got_ref, msg_ref, later_ref, msg_out, later_out):
    heads = got_ref.shape[0]
    lanes = got_ref.shape[2]
    valid = flag_ref[...]
    got_b = got_ref[:, 0:P_SIZE, :] * valid
    got_a = got_ref[:, P_SIZE : P_SIZE + 1, :] * valid + (1.0 - valid)
    later_a = later_ref[:, P_SIZE : P_SIZE + 1, :]
    later_out[:, 0:P_SIZE, :] = later_ref[:, 0:P_SIZE, :] + later_a * got_b
    later_out[:, P_SIZE : P_SIZE + 8, :] = jnp.broadcast_to(later_a * got_a, (heads, 8, lanes))
    whole_a = msg_ref[:, P_SIZE : P_SIZE + 1, :]
    msg_out[:, 0:P_SIZE, :] = msg_ref[:, 0:P_SIZE, :] + whole_a * got_b
    msg_out[:, P_SIZE : P_SIZE + 8, :] = jnp.broadcast_to(whole_a * got_a, (heads, 8, lanes))
    msg_out[:, P_SIZE + 8 :, :] = msg_ref[:, P_SIZE + 8 :, :] + got_ref[:, P_SIZE + 8 :, :]


def on_device(
    prompt_grad,
    prompt_keys,
    prompt_queries,
    prompt_decay,
    resp_grad,
    resp_keys,
    resp_queries,
    resp_decay,
    resp_segment,
):
    resp_alive = resp_segment < RESP_DEV
    resp_parts = group_parts(resp_grad, resp_queries, resp_decay, resp_segment, resp_alive)
    resp_dx = group_output(resp_keys, resp_queries, resp_parts).astype(jnp.bfloat16)
    partial_state = initial_state(
        resp_grad, resp_queries, resp_decay, resp_segment, resp_alive, resp_parts[0]
    )
    resp_len = lax.axis_size("resp")
    head_count = prompt_decay.shape[0]
    prompt_len = prompt_grad.shape[0]
    zero_label = jnp.zeros((prompt_len,), jnp.int32)
    all_alive = jnp.ones((prompt_len,), jnp.bool_)
    prompt_parts = group_parts(prompt_grad, prompt_queries, prompt_decay, zero_label, all_alive)
    cum_sums = prompt_parts[0]
    start_grad = prompt_parts[7]
    shard_total = cum_sums[:, -1]
    seq_index = lax.axis_index("seq")
    seq_len = lax.axis_size("seq")
    share = head_count // partial_state.shape[0]
    pairs = []
    for src_seq in range(seq_len):
        for src_resp in range(resp_len):
            dst_seq = share * src_resp + src_seq % share
            dst_resp = src_seq // share
            pairs.append((src_seq * resp_len + src_resp, dst_seq * resp_len + dst_resp))
    piece = lax.ppermute(partial_state, ("seq", "resp"), pairs)
    own_a = jnp.exp(shard_total)
    slotted = lax.dynamic_update_slice_in_dim(
        jnp.zeros((head_count,) + partial_state.shape[1:], jnp.float32),
        piece,
        (seq_index % share) * partial_state.shape[0],
        0,
    )
    message = jnp.concatenate(
        [start_grad, jnp.broadcast_to(own_a[:, None, None], (head_count, 8, N)), slotted], axis=1
    )
    later = jnp.concatenate(
        [jnp.zeros_like(start_grad), jnp.ones((head_count, 8, N), jnp.float32)], axis=1
    )
    step = pl.pallas_call(
        _scan_round,
        out_shape=(
            jax.ShapeDtypeStruct(message.shape, jnp.float32),
            jax.ShapeDtypeStruct(later.shape, jnp.float32),
        ),
        interpret=_INTERPRET,
    )
    shift = 1
    while shift < seq_len:
        pairs = [((k + shift) % seq_len, k) for k in range(seq_len)]
        got = lax.ppermute(message, "seq", pairs)
        flag = jnp.broadcast_to(
            (seq_index + shift < seq_len).astype(jnp.float32), (1, 1, N)
        )
        message, later = step(flag, got, message, later)
        shift *= 2
    incoming = later[:, :P_SIZE] + later[:, P_SIZE : P_SIZE + 1] * message[:, P_SIZE + 8 :]
    local_part = group_output(prompt_keys, prompt_queries, prompt_parts)
    carry_term = jnp.einsum(
        "hpn,tn->thp",
        incoming.astype(jnp.bfloat16),
        prompt_keys,
        preferred_element_type=jnp.float32,
    )
    carry_term = carry_term * jnp.exp(shard_total[:, None] - cum_sums).T[:, :, None]
    prompt_dx = (local_part + carry_term.reshape(prompt_len, head_count * P_SIZE)).astype(
        jnp.bfloat16
    )
    return (prompt_dx, resp_dx)


def solution(mesh):
    return jax.shard_map(
        on_device,
        mesh=mesh,
        in_specs=(
            P("seq", "resp"),
            P("seq", None),
            P("seq", None),
            P("resp", "seq"),
            P("resp", "seq"),
            P("resp", None),
            P("resp", None),
            P("seq", "resp"),
            P("resp"),
        ),
        out_specs=(P("seq", "resp"), P("resp", "seq")),
        check_vma=False,
    )
```

```python
import jax
import jax.numpy as jnp
from jax import lax
from jax.sharding import PartitionSpec as P

P_SIZE = 64
N = 128
GROUP = 256
RESP_DEV = 8


def group_parts(out_grad, queries, decay, segment, alive_mask):
    tokens = out_grad.shape[0]
    head_count = decay.shape[0]
    groups = tokens // GROUP
    cum_sums = jnp.cumsum(decay, axis=1)
    cum_group = cum_sums.reshape(head_count, groups, GROUP).transpose(1, 0, 2)
    decay_group = decay.reshape(head_count, groups, GROUP).transpose(1, 0, 2)
    before = cum_group[:, :, 0] - decay_group[:, :, 0]
    seg_group = segment.reshape(groups, GROUP)
    alive_group = alive_mask.reshape(groups, GROUP)
    first_label = seg_group[:, 0]
    last_label = seg_group[:, -1]
    grad_group = out_grad.reshape(groups, GROUP, head_count, P_SIZE)
    query_group = queries.reshape(groups, GROUP, N)
    keep_mask = (seg_group == first_label[:, None]) & alive_group
    factor = jnp.where(keep_mask[:, None, :], jnp.exp(cum_group - before[:, :, None]), 0.0)
    weighted = (factor.transpose(0, 2, 1)[:, :, :, None] * grad_group).astype(jnp.bfloat16)
    states = jnp.einsum("clhp,cln->chpn", weighted, query_group, preferred_element_type=jnp.float32)
    group_gains = jnp.exp(cum_group[:, :, -1] - before)
    joined = (first_label == last_label).astype(jnp.float32)
    linked = jnp.concatenate(
        [jnp.ones((1,), jnp.float32), (last_label[:-1] == first_label[1:]).astype(jnp.float32)]
    )

    flow = joined[:, None] * group_gains * jnp.concatenate(
        [linked[1:], jnp.zeros((1,), jnp.float32)]
    )[:, None]
    carry_at = jnp.arange(groups + 1)[:, None, None]
    state_at = jnp.arange(groups)[None, :, None]
    step_at = jnp.arange(groups)[None, None, :]
    inside = (carry_at <= step_at) & (step_at < state_at)
    spans = jnp.prod(jnp.where(inside[None], flow.T[:, None, None, :], 1.0), axis=3)
    link_at = jnp.concatenate([linked, jnp.zeros((1,), jnp.float32)])
    coef = jnp.where((carry_at[:, :, 0] <= state_at[:, :, 0])[None], spans, 0.0) * link_at[None, :, None]
    carries = jnp.einsum(
        "hcd,dhpn->chpn", coef, states, precision=lax.Precision.HIGHEST
    )
    start_grad = carries[0]
    end_grads = carries[1:]
    return (
        cum_sums,
        cum_group,
        seg_group,
        alive_group,
        last_label,
        grad_group,
        end_grads,
        start_grad,
    )


def group_output(key_rows, queries, parts):
    cum_sums, cum_group, seg_group, alive_group, last_label, grad_group, end_grads, start_grad = (
        parts
    )
    groups = seg_group.shape[0]
    head_count = cum_group.shape[1]
    key_group = key_rows.reshape(groups, GROUP, N)
    query_group = queries.reshape(groups, GROUP, N)
    scores = jnp.einsum("csn,ctn->cst", query_group, key_group, preferred_element_type=jnp.float32)
    row_index = lax.broadcasted_iota(jnp.int32, (GROUP, GROUP), 0)
    col_index = lax.broadcasted_iota(jnp.int32, (GROUP, GROUP), 1)
    keep_mask = (
        (row_index >= col_index)[None]
        & (seg_group[:, :, None] == seg_group[:, None, :])
        & alive_group[:, :, None]
    )
    spread = cum_group[:, :, :, None] - cum_group[:, :, None, :]
    decays = jnp.exp(jnp.where(keep_mask[:, None], spread, -jnp.inf))
    mixing = (scores[:, None] * decays).astype(jnp.bfloat16)
    inner_part = jnp.einsum(
        "chst,cshp->cthp", mixing, grad_group, preferred_element_type=jnp.float32
    )
    across = jnp.einsum(
        "chpn,ctn->cthp",
        end_grads.astype(jnp.bfloat16),
        key_group,
        preferred_element_type=jnp.float32,
    )
    reach_weight = jnp.where(
        (seg_group == last_label[:, None])[:, None, :],
        jnp.exp(cum_group[:, :, -1:] - cum_group),
        0.0,
    )
    summed_parts = inner_part + across * reach_weight.transpose(0, 2, 1)[:, :, :, None]
    return summed_parts.reshape(groups * GROUP, head_count * P_SIZE)


def initial_state(out_grad, queries, decay, segment, alive_mask, cum_sums):
    tokens = out_grad.shape[0]
    head_count = decay.shape[0]
    firsts = jnp.concatenate([jnp.ones((1,), jnp.bool_), segment[1:] != segment[:-1]])
    labels = jnp.arange(RESP_DEV + 1, dtype=jnp.int32)
    member = segment[:, None] == labels[None, :]
    opening = cum_sums - decay
    base_label = jnp.sum(
        jnp.where((member & firsts[:, None])[None], opening[:, :, None], 0.0), axis=1
    )
    base_token = jnp.sum(jnp.where(member[None], base_label[:, None, :], 0.0), axis=2)
    factor = jnp.where(alive_mask[None], jnp.exp(cum_sums - base_token), 0.0)
    weighted = (factor.T[:, :, None] * out_grad.reshape(tokens, head_count, P_SIZE)).astype(
        jnp.bfloat16
    )
    return jnp.einsum("thp,tn->hpn", weighted, queries, preferred_element_type=jnp.float32)


def on_device(
    prompt_grad,
    prompt_keys,
    prompt_queries,
    prompt_decay,
    resp_grad,
    resp_keys,
    resp_queries,
    resp_decay,
    resp_segment,
):
    resp_alive = resp_segment < RESP_DEV
    resp_parts = group_parts(resp_grad, resp_queries, resp_decay, resp_segment, resp_alive)
    resp_dx = group_output(resp_keys, resp_queries, resp_parts).astype(jnp.bfloat16)
    partial_state = initial_state(
        resp_grad, resp_queries, resp_decay, resp_segment, resp_alive, resp_parts[0]
    )
    resp_len = lax.axis_size("resp")
    head_count = prompt_decay.shape[0]
    prompt_len = prompt_grad.shape[0]
    zero_label = jnp.zeros((prompt_len,), jnp.int32)
    all_alive = jnp.ones((prompt_len,), jnp.bool_)
    prompt_parts = group_parts(prompt_grad, prompt_queries, prompt_decay, zero_label, all_alive)
    cum_sums = prompt_parts[0]
    start_grad = prompt_parts[7]
    shard_total = cum_sums[:, -1]
    seq_index = lax.axis_index("seq")
    seq_len = lax.axis_size("seq")
    share = head_count // partial_state.shape[0]
    pairs = []
    for src_seq in range(seq_len):
        for src_resp in range(resp_len):
            dst_seq = share * src_resp + src_seq % share
            dst_resp = src_seq // share
            pairs.append((src_seq * resp_len + src_resp, dst_seq * resp_len + dst_resp))
    pieces = lax.ppermute(partial_state, ("seq", "resp"), pairs)[None]
    local_part = group_output(prompt_keys, prompt_queries, prompt_parts)
    start_grad, resp_dx, local_part = lax.optimization_barrier((start_grad, resp_dx, local_part))
    whole_b = start_grad
    whole_a = jnp.exp(shard_total)
    later_b = jnp.zeros_like(start_grad)
    later_a = jnp.ones_like(whole_a)
    my_heads = None
    shift = 1
    while shift < seq_len:
        pairs = [((k + shift) % seq_len, k) for k in range(seq_len)]
        parts = [whole_b, jnp.broadcast_to(whole_a[:, None, None], (head_count, 1, N))]
        if my_heads is None:
            parts.append(pieces.reshape(head_count, -1, N))
        else:
            parts.append(my_heads)
        got = lax.ppermute(jnp.concatenate(parts, axis=1), "seq", pairs)
        valid = seq_index + shift < seq_len
        got_b = jnp.where(valid, got[:, :P_SIZE], 0.0)
        got_a = jnp.where(valid, got[:, P_SIZE, 0], 1.0)
        rest = got[:, P_SIZE + 1 :]
        if my_heads is None:
            pieces = jnp.concatenate([pieces, rest.reshape(pieces.shape)], axis=0)
            if pieces.shape[0] == share:
                order = (jnp.arange(share) - seq_index % share) % share
                my_heads = jnp.take(pieces, order, axis=0).reshape(
                    (head_count,) + partial_state.shape[1:]
                )
        else:
            my_heads = my_heads + rest
        later_b = later_b + later_a[:, None, None] * got_b
        later_a = later_a * got_a
        if shift * 2 < seq_len:
            whole_b = whole_b + whole_a[:, None, None] * got_b
            whole_a = whole_a * got_a
        shift *= 2
    incoming = later_b + later_a[:, None, None] * my_heads
    carry_term = jnp.einsum(
        "hpn,tn->thp",
        incoming.astype(jnp.bfloat16),
        prompt_keys,
        preferred_element_type=jnp.float32,
    )
    carry_term = carry_term * jnp.exp(shard_total[:, None] - cum_sums).T[:, :, None]
    prompt_dx = (local_part + carry_term.reshape(prompt_len, head_count * P_SIZE)).astype(
        jnp.bfloat16
    )
    return (prompt_dx, resp_dx)


def solution(mesh):
    return jax.shard_map(
        on_device,
        mesh=mesh,
        in_specs=(
            P("seq", "resp"),
            P("seq", None),
            P("seq", None),
            P("resp", "seq"),
            P("resp", "seq"),
            P("resp", None),
            P("resp", None),
            P("seq", "resp"),
            P("resp"),
        ),
        out_specs=(P("seq", "resp"), P("resp", "seq")),
        check_vma=False,
    )
```

```python
import jax
import jax.numpy as jnp
from jax import lax
from jax.sharding import PartitionSpec as P

P_SIZE = 64
N = 128
GROUP = 256
RESP_DEV = 8


def group_parts(out_grad, queries, decay, segment, alive_mask):
    tokens = out_grad.shape[0]
    head_count = decay.shape[0]
    groups = tokens // GROUP
    cum_sums = jnp.cumsum(decay, axis=1)
    cum_group = cum_sums.reshape(head_count, groups, GROUP).transpose(1, 0, 2)
    decay_group = decay.reshape(head_count, groups, GROUP).transpose(1, 0, 2)
    before = cum_group[:, :, 0] - decay_group[:, :, 0]
    seg_group = segment.reshape(groups, GROUP)
    alive_group = alive_mask.reshape(groups, GROUP)
    first_label = seg_group[:, 0]
    last_label = seg_group[:, -1]
    grad_group = out_grad.reshape(groups, GROUP, head_count, P_SIZE)
    query_group = queries.reshape(groups, GROUP, N)
    keep_mask = (seg_group == first_label[:, None]) & alive_group
    factor = jnp.where(keep_mask[:, None, :], jnp.exp(cum_group - before[:, :, None]), 0.0)
    weighted = (factor.transpose(0, 2, 1)[:, :, :, None] * grad_group).astype(jnp.bfloat16)
    states = jnp.einsum("clhp,cln->chpn", weighted, query_group, preferred_element_type=jnp.float32)
    group_gains = jnp.exp(cum_group[:, :, -1] - before)
    joined = (first_label == last_label).astype(jnp.float32)
    linked = jnp.concatenate(
        [jnp.ones((1,), jnp.float32), (last_label[:-1] == first_label[1:]).astype(jnp.float32)]
    )

    flow = joined[:, None] * group_gains * jnp.concatenate(
        [linked[1:], jnp.zeros((1,), jnp.float32)]
    )[:, None]
    carry_at = jnp.arange(groups + 1)[:, None, None]
    state_at = jnp.arange(groups)[None, :, None]
    step_at = jnp.arange(groups)[None, None, :]
    inside = (carry_at <= step_at) & (step_at < state_at)
    spans = jnp.prod(jnp.where(inside[None], flow.T[:, None, None, :], 1.0), axis=3)
    link_at = jnp.concatenate([linked, jnp.zeros((1,), jnp.float32)])
    coef = jnp.where((carry_at[:, :, 0] <= state_at[:, :, 0])[None], spans, 0.0) * link_at[None, :, None]
    carries = jnp.einsum(
        "hcd,dhpn->chpn", coef, states, precision=lax.Precision.HIGHEST
    )
    start_grad = carries[0]
    end_grads = carries[1:]
    return (
        cum_sums,
        cum_group,
        seg_group,
        alive_group,
        last_label,
        grad_group,
        end_grads,
        start_grad,
    )


def group_output(key_rows, queries, parts):
    cum_sums, cum_group, seg_group, alive_group, last_label, grad_group, end_grads, start_grad = (
        parts
    )
    groups = seg_group.shape[0]
    head_count = cum_group.shape[1]
    key_group = key_rows.reshape(groups, GROUP, N)
    query_group = queries.reshape(groups, GROUP, N)
    scores = jnp.einsum("csn,ctn->cst", query_group, key_group, preferred_element_type=jnp.float32)
    row_index = lax.broadcasted_iota(jnp.int32, (GROUP, GROUP), 0)
    col_index = lax.broadcasted_iota(jnp.int32, (GROUP, GROUP), 1)
    keep_mask = (
        (row_index >= col_index)[None]
        & (seg_group[:, :, None] == seg_group[:, None, :])
        & alive_group[:, :, None]
    )
    spread = cum_group[:, :, :, None] - cum_group[:, :, None, :]
    decays = jnp.exp(jnp.where(keep_mask[:, None], spread, -jnp.inf))
    mixing = (scores[:, None] * decays).astype(jnp.bfloat16)
    inner_part = jnp.einsum(
        "chst,cshp->cthp", mixing, grad_group, preferred_element_type=jnp.float32
    )
    across = jnp.einsum(
        "chpn,ctn->cthp",
        end_grads.astype(jnp.bfloat16),
        key_group,
        preferred_element_type=jnp.float32,
    )
    reach_weight = jnp.where(
        (seg_group == last_label[:, None])[:, None, :],
        jnp.exp(cum_group[:, :, -1:] - cum_group),
        0.0,
    )
    summed_parts = inner_part + across * reach_weight.transpose(0, 2, 1)[:, :, :, None]
    return summed_parts.reshape(groups * GROUP, head_count * P_SIZE)


def initial_state(out_grad, queries, decay, segment, alive_mask, cum_sums):
    tokens = out_grad.shape[0]
    head_count = decay.shape[0]
    firsts = jnp.concatenate([jnp.ones((1,), jnp.bool_), segment[1:] != segment[:-1]])
    labels = jnp.arange(RESP_DEV + 1, dtype=jnp.int32)
    member = segment[:, None] == labels[None, :]
    opening = cum_sums - decay
    base_label = jnp.sum(
        jnp.where((member & firsts[:, None])[None], opening[:, :, None], 0.0), axis=1
    )
    base_token = jnp.sum(jnp.where(member[None], base_label[:, None, :], 0.0), axis=2)
    factor = jnp.where(alive_mask[None], jnp.exp(cum_sums - base_token), 0.0)
    weighted = (factor.T[:, :, None] * out_grad.reshape(tokens, head_count, P_SIZE)).astype(
        jnp.bfloat16
    )
    return jnp.einsum("thp,tn->hpn", weighted, queries, preferred_element_type=jnp.float32)


def on_device(
    prompt_grad,
    prompt_keys,
    prompt_queries,
    prompt_decay,
    resp_grad,
    resp_keys,
    resp_queries,
    resp_decay,
    resp_segment,
):
    resp_alive = resp_segment < RESP_DEV
    resp_parts = group_parts(resp_grad, resp_queries, resp_decay, resp_segment, resp_alive)
    resp_dx = group_output(resp_keys, resp_queries, resp_parts).astype(jnp.bfloat16)
    partial_state = initial_state(
        resp_grad, resp_queries, resp_decay, resp_segment, resp_alive, resp_parts[0]
    )
    resp_len = lax.axis_size("resp")
    head_count = prompt_decay.shape[0]
    prompt_len = prompt_grad.shape[0]
    zero_label = jnp.zeros((prompt_len,), jnp.int32)
    all_alive = jnp.ones((prompt_len,), jnp.bool_)
    prompt_parts = group_parts(prompt_grad, prompt_queries, prompt_decay, zero_label, all_alive)
    cum_sums = prompt_parts[0]
    start_grad = prompt_parts[7]
    shard_total = cum_sums[:, -1]
    seq_index = lax.axis_index("seq")
    seq_len = lax.axis_size("seq")
    share = head_count // partial_state.shape[0]
    pairs = []
    for src_seq in range(seq_len):
        for src_resp in range(resp_len):
            dst_seq = share * src_resp + src_seq % share
            dst_resp = src_seq // share
            pairs.append((src_seq * resp_len + src_resp, dst_seq * resp_len + dst_resp))
    shift = 1
    while shift < resp_len:
        partial_state = partial_state + lax.ppermute(
            partial_state, "resp", [(k, k ^ shift) for k in range(resp_len)]
        )
        shift *= 2
    pieces = lax.ppermute(partial_state, ("seq", "resp"), pairs)[None]
    whole_b = start_grad
    whole_a = jnp.exp(shard_total)
    later_b = jnp.zeros_like(start_grad)
    later_a = jnp.ones_like(whole_a)
    my_heads = None
    shift = 1
    while shift < seq_len:
        pairs = [((k + shift) % seq_len, k) for k in range(seq_len)]
        parts = [whole_b, jnp.broadcast_to(whole_a[:, None, None], (head_count, 1, N))]
        if my_heads is None:
            parts.append(pieces.reshape(head_count, -1, N))
        got = lax.ppermute(jnp.concatenate(parts, axis=1), "seq", pairs)
        valid = seq_index + shift < seq_len
        got_b = jnp.where(valid, got[:, :P_SIZE], 0.0)
        got_a = jnp.where(valid, got[:, P_SIZE, 0], 1.0)
        rest = got[:, P_SIZE + 1 :]
        if my_heads is None:
            pieces = jnp.concatenate([pieces, rest.reshape(pieces.shape)], axis=0)
            if pieces.shape[0] == share:
                order = (jnp.arange(share) - seq_index % share) % share
                my_heads = jnp.take(pieces, order, axis=0).reshape(
                    (head_count,) + partial_state.shape[1:]
                )
        later_b = later_b + later_a[:, None, None] * got_b
        later_a = later_a * got_a
        if shift * 2 < seq_len:
            whole_b = whole_b + whole_a[:, None, None] * got_b
            whole_a = whole_a * got_a
        shift *= 2
    incoming = later_b + later_a[:, None, None] * my_heads
    local_part = group_output(prompt_keys, prompt_queries, prompt_parts)
    carry_term = jnp.einsum(
        "hpn,tn->thp",
        incoming.astype(jnp.bfloat16),
        prompt_keys,
        preferred_element_type=jnp.float32,
    )
    carry_term = carry_term * jnp.exp(shard_total[:, None] - cum_sums).T[:, :, None]
    prompt_dx = (local_part + carry_term.reshape(prompt_len, head_count * P_SIZE)).astype(
        jnp.bfloat16
    )
    return (prompt_dx, resp_dx)


def solution(mesh):
    return jax.shard_map(
        on_device,
        mesh=mesh,
        in_specs=(
            P("seq", "resp"),
            P("seq", None),
            P("seq", None),
            P("resp", "seq"),
            P("resp", "seq"),
            P("resp", None),
            P("resp", None),
            P("seq", "resp"),
            P("resp"),
        ),
        out_specs=(P("seq", "resp"), P("resp", "seq")),
        check_vma=False,
    )
```
